32 devices in a mesh: grp: 2 (over y), seq: 16 (over z, x, core).
Axes of the slice: x: 2, y: 2, z: 4, core: 2. Of those that a mesh axis runs over, the one named last changes fastest.
Arguments:
- activations: bfloat16 [131072, 256], P(('grp', 'seq')), parts along dimension 0, may hold values from -6 to 6
- cotangent: bfloat16 [131072, 256], P(('grp', 'seq')), parts along dimension 0, may hold values from -6 to 6
- conv_weight: bfloat16 [768, 512], replicated, may hold values from -0.21875 to 0.21875
- out_weight: bfloat16 [256, 256], replicated, may hold values from -0.375 to 0.375
Outputs:
- grad_input: bfloat16 [131072, 256], P(('grp', 'seq')), parts along dimension 0
- grad_conv: float32 [1536, 512], P('grp'), parts along dimension 0
- grad_out: float32 [512, 256], P('grp'), parts along dimension 0
The draws below stay inside these ranges and needn't reach their ends.
There are 2 independent parts, one for each index of `grp`. The reference program is written for one: setup_inputs(seed, part) draws one part's arguments, and reference() takes and returns one part's arrays. A program takes and returns all parts, laid end to end along the dimension named above; an argument that names none is the same for every part. Nothing has to cross between parts.
All inputs are finite; a program needn't handle non-finite values.
Results may differ from the reference program's by a relative error of at most 0.0032.
Values may be sent and summed in bfloat16 or wider, within the bound.
No kernel may reach another device: no remote copies, remote signals or barrier semaphores. Data moves between devices by JAX's collectives and lax.ppermute only.
A program may use at most 128 MiB of HBM per device.

```python
import jax
import jax.numpy as jnp
from jax import lax

CHANNEL_COUNT = 256
DEVICE_POSITIONS = 4096
TAP_SPACING = 16384
SEQ_LEN = 65536


def levels(key, extent, cuts, smallest, largest):
    gain, own = 1.0, jax.random.fold_in(key, 6)
    for position, parts in cuts:
        steps = jnp.exp(jax.random.uniform(jax.random.fold_in(own, position), (parts,), jnp.float32, smallest / len(cuts), largest / len(cuts)))
        gain = gain * jnp.repeat(steps, extent[position] // parts).reshape([-1 if axis == position else 1 for axis in range(len(extent))])
    return gain


def gaussian(key, extent, deviation, bound, cuts=(), kind=jnp.bfloat16):
    entries = deviation * jax.random.normal(key, extent, jnp.float32)
    if cuts:
        entries = entries * levels(key, extent, cuts, -0.22, 0.18)
    return jnp.clip(entries, -bound, bound).astype(kind)


def setup_inputs(seed: int = 0, part: int = 0) -> dict:
    splits = jax.random.split(jax.random.key(seed), 5)
    part_keys = jax.random.split(jax.random.fold_in(splits[4], part), 5)
    return {
        "activations": gaussian(part_keys[0], (SEQ_LEN, CHANNEL_COUNT), 1.0, 6.0, ((0, 16),)),
        "cotangent": gaussian(part_keys[1], (SEQ_LEN, CHANNEL_COUNT), 1.0, 6.0, ((0, 16),)),
        "conv_weight": gaussian(splits[2], (3 * CHANNEL_COUNT, 2 * CHANNEL_COUNT), (3 * CHANNEL_COUNT) ** -0.5, 0.21875),
        "out_weight": gaussian(splits[3], (CHANNEL_COUNT, CHANNEL_COUNT), CHANNEL_COUNT ** -0.5, 0.375),
    }


def local_layer(left_tap_input, middle, right_tap_input, grad_in, conv_weight, out_weight):
    channels = middle.shape[1]
    w_low = conv_weight[:channels]
    w_mid = conv_weight[channels:2 * channels]
    w_high = conv_weight[2 * channels:]
    preact = jnp.dot(left_tap_input, w_low, preferred_element_type=jnp.float32)
    preact = preact + jnp.dot(middle, w_mid, preferred_element_type=jnp.float32)
    preact = preact + jnp.dot(right_tap_input, w_high, preferred_element_type=jnp.float32)
    tanh_part = jnp.tanh(preact[:, :channels])
    sigm_part = jax.nn.sigmoid(preact[:, channels:])
    gated_out = (tanh_part * sigm_part).astype(jnp.bfloat16)
    grad_wout = jnp.dot(gated_out.T, grad_in, preferred_element_type=jnp.float32)
    grad_gated = jnp.dot(grad_in, out_weight.T, preferred_element_type=jnp.float32)
    grad_filt = grad_gated * sigm_part * (1.0 - tanh_part * tanh_part)
    grad_gate = grad_gated * tanh_part * sigm_part * (1.0 - sigm_part)
    grad_pre = jnp.concatenate([grad_filt, grad_gate], axis=1).astype(jnp.bfloat16)
    grad_wconv = jnp.concatenate([jnp.dot(left_tap_input.T, grad_pre, preferred_element_type=jnp.float32), jnp.dot(middle.T, grad_pre, preferred_element_type=jnp.float32), jnp.dot(right_tap_input.T, grad_pre, preferred_element_type=jnp.float32)], axis=0)
    lower_term = jnp.dot(grad_pre, w_low.T, preferred_element_type=jnp.float32).astype(jnp.bfloat16)
    term_mid = jnp.dot(grad_pre, w_mid.T, preferred_element_type=jnp.float32)
    upper_term = jnp.dot(grad_pre, w_high.T, preferred_element_type=jnp.float32).astype(jnp.bfloat16)
    return (grad_wconv, grad_wout, lower_term, term_mid, upper_term)

def reference(activations, cotangent, conv_weight, out_weight):
    block_list = SEQ_LEN // DEVICE_POSITIONS
    left_tap_input = jnp.roll(activations, TAP_SPACING, axis=0).reshape(block_list, DEVICE_POSITIONS, CHANNEL_COUNT)
    right_tap_input = jnp.roll(activations, -TAP_SPACING, axis=0).reshape(block_list, DEVICE_POSITIONS, CHANNEL_COUNT)
    middle = activations.reshape(block_list, DEVICE_POSITIONS, CHANNEL_COUNT)
    grad_in = cotangent.reshape(block_list, DEVICE_POSITIONS, CHANNEL_COUNT)

    def block_step(running, pieces):
        left_block, mid_block, right_block, grad_block = pieces
        grad_wconv, grad_wout, lower_term, term_mid, upper_term = local_layer(left_block, mid_block, right_block, grad_block, conv_weight, out_weight)
        base_part = grad_block.astype(jnp.float32) + term_mid
        return ((running[0] + grad_wconv, running[1] + grad_wout), (base_part, lower_term, upper_term))
    start = (jnp.zeros((3 * CHANNEL_COUNT, 2 * CHANNEL_COUNT), jnp.float32), jnp.zeros((CHANNEL_COUNT, CHANNEL_COUNT), jnp.float32))
    sums, outs_all = lax.scan(block_step, start, (left_tap_input, middle, right_tap_input, grad_in))
    base_part, lower_term, upper_term = outs_all
    lower_term = lax.optimization_barrier(lower_term.reshape(SEQ_LEN, CHANNEL_COUNT))
    upper_term = lax.optimization_barrier(upper_term.reshape(SEQ_LEN, CHANNEL_COUNT))
    total_sum = base_part.reshape(SEQ_LEN, CHANNEL_COUNT)
    total_sum = total_sum + jnp.roll(lower_term, -TAP_SPACING, axis=0).astype(jnp.float32)
    total_sum = total_sum + jnp.roll(upper_term, TAP_SPACING, axis=0).astype(jnp.float32)
    norm_factor = 1.0 / jnp.sqrt(jnp.float32(SEQ_LEN))
    return (total_sum.astype(jnp.bfloat16), sums[0] * norm_factor, sums[1] * norm_factor)
```

```python
import math

import jax
import jax.numpy as jnp
from jax import lax
from jax.sharding import PartitionSpec as P

TAP_SPACING = 16384
CHUNKS = 4


def from_behind(value, axis, steps):
    count = lax.axis_size(axis)
    pairs = [(source, (source + steps) % count) for source in range(count)]
    return lax.ppermute(value, axis, pairs)


def exchange(value, axis, bit):
    count = lax.axis_size(axis)
    pairs = [(source, source ^ bit) for source in range(count)]
    return lax.ppermute(value, axis, pairs)


def all_reduce_sum(flat, axis, scale):
    count = lax.axis_size(axis)
    idx = lax.axis_index(axis)
    bits = []
    bit = 1
    while bit < count:
        bits.append(bit)
        bit *= 2
    buf = flat
    for bit in bits:
        half = buf.shape[0] // 2
        upper = (idx // bit) % 2
        mine = lax.dynamic_slice_in_dim(buf, upper * half, half)
        theirs = lax.dynamic_slice_in_dim(buf, (1 - upper) * half, half)
        buf = mine + exchange(theirs, axis, bit)
    buf = buf * scale
    for bit in reversed(bits):
        upper = (idx // bit) % 2
        other = exchange(buf, axis, bit)
        lo = jnp.where(upper == 1, other, buf)
        hi = jnp.where(upper == 1, buf, other)
        buf = jnp.concatenate([lo, hi])
    return buf


def chunk_layer(left_tap_input, middle, right_tap_input, grad_in, conv_weight, out_weight):
    channels = middle.shape[1]
    w_low = conv_weight[:channels]
    w_mid = conv_weight[channels : 2 * channels]
    w_high = conv_weight[2 * channels :]
    preact = jnp.dot(left_tap_input, w_low, preferred_element_type=jnp.float32)
    preact = preact + jnp.dot(middle, w_mid, preferred_element_type=jnp.float32)
    preact = preact + jnp.dot(right_tap_input, w_high, preferred_element_type=jnp.float32)
    tanh_part = jnp.tanh(preact[:, :channels])
    sigm_part = jax.nn.sigmoid(preact[:, channels:])
    gated_out = (tanh_part * sigm_part).astype(jnp.bfloat16)
    first_dims = (((0,), (0,)), ((), ()))
    last_dims = (((1,), (1,)), ((), ()))
    grad_wout = lax.dot_general(gated_out, grad_in, first_dims, preferred_element_type=jnp.float32)
    grad_gated = lax.dot_general(grad_in, out_weight, last_dims, preferred_element_type=jnp.float32)
    grad_filt = grad_gated * sigm_part * (1.0 - tanh_part * tanh_part)
    grad_gate = grad_gated * tanh_part * sigm_part * (1.0 - sigm_part)
    grad_pre = jnp.concatenate([grad_filt, grad_gate], axis=1).astype(jnp.bfloat16)
    grad_wconv = jnp.concatenate(
        [
            lax.dot_general(left_tap_input, grad_pre, first_dims, preferred_element_type=jnp.float32),
            lax.dot_general(middle, grad_pre, first_dims, preferred_element_type=jnp.float32),
            lax.dot_general(right_tap_input, grad_pre, first_dims, preferred_element_type=jnp.float32),
        ],
        axis=0,
    )
    lower_term = lax.dot_general(grad_pre, w_low, last_dims, preferred_element_type=jnp.float32).astype(jnp.bfloat16)
    term_mid = lax.dot_general(grad_pre, w_mid, last_dims, preferred_element_type=jnp.float32)
    upper_term = lax.dot_general(grad_pre, w_high, last_dims, preferred_element_type=jnp.float32).astype(jnp.bfloat16)
    return grad_wconv, grad_wout, lower_term, term_mid, upper_term


def body(activations, cotangent, conv_weight, out_weight):
    positions, channels = activations.shape
    seq_size = lax.axis_size("seq")
    spacing = TAP_SPACING // positions
    rows = positions // CHUNKS
    wconv_total = None
    wout_total = None
    outs = []
    for k in range(CHUNKS):
        middle = activations[k * rows : (k + 1) * rows]
        grad_in = cotangent[k * rows : (k + 1) * rows]
        left_tap_input = from_behind(middle, "seq", spacing)
        right_tap_input = from_behind(middle, "seq", -spacing)
        grad_wconv, grad_wout, lower_term, term_mid, upper_term = chunk_layer(
            left_tap_input, middle, right_tap_input, grad_in, conv_weight, out_weight
        )
        wconv_total = grad_wconv if wconv_total is None else wconv_total + grad_wconv
        wout_total = grad_wout if wout_total is None else wout_total + grad_wout
        received_ahead = from_behind(lower_term, "seq", -spacing)
        received_behind = from_behind(upper_term, "seq", spacing)
        total_sum = grad_in.astype(jnp.float32) + term_mid
        total_sum = total_sum + received_ahead.astype(jnp.float32) + received_behind.astype(jnp.float32)
        outs.append(total_sum.astype(jnp.bfloat16))
    grad_input = jnp.concatenate(outs, axis=0)
    norm_factor = 1.0 / math.sqrt(positions * seq_size)
    flat = jnp.concatenate([wconv_total.reshape(-1), wout_total.reshape(-1)])
    summed = all_reduce_sum(flat, "seq", jnp.float32(norm_factor))
    split = wconv_total.size
    grad_conv = summed[:split].reshape(wconv_total.shape)
    grad_out = summed[split:].reshape(wout_total.shape)
    return grad_input, grad_conv, grad_out


def solution(mesh):
    in_specs = (P(("grp", "seq"), None), P(("grp", "seq"), None), P(), P())
    out_specs = (P(("grp", "seq"), None), P("grp", None), P("grp", None))
    return jax.shard_map(body, mesh=mesh, in_specs=in_specs, out_specs=out_specs, check_vma=False)
```

```python
import math

import jax
import jax.numpy as jnp
from jax import lax
from jax.sharding import PartitionSpec as P

TAP_SPACING = 16384
CHUNKS = 4
TERM_PIECES = 4


def from_behind(value, axis, steps):
    count = lax.axis_size(axis)
    pairs = [(source, (source + steps) % count) for source in range(count)]
    return lax.ppermute(value, axis, pairs)


def exchange(value, axis, bit):
    count = lax.axis_size(axis)
    pairs = [(source, source ^ bit) for source in range(count)]
    return lax.ppermute(value, axis, pairs)


def all_reduce_sum(flat, axis, scale, riders):
    count = lax.axis_size(axis)
    idx = lax.axis_index(axis)
    bits = []
    bit = 1
    while bit < count:
        bits.append(bit)
        bit *= 2
    steps = [(bit, True) for bit in bits] + [(bit, False) for bit in reversed(bits)]
    per_rider = -(-len(steps) // max(len(riders), 1))
    results = []
    buf = flat
    for number, (bit, down) in enumerate(steps):
        if riders and number % per_rider == 0:
            if results:
                buf, results[-1] = lax.optimization_barrier((buf, results[-1]))
            results.append(riders[len(results)]())
        upper = (idx // bit) % 2
        if down:
            half = buf.shape[0] // 2
            mine = lax.dynamic_slice_in_dim(buf, upper * half, half)
            theirs = lax.dynamic_slice_in_dim(buf, (1 - upper) * half, half)
            buf = mine + exchange(theirs, axis, bit)
            if number == len(bits) - 1:
                buf = buf * scale
        else:
            other = exchange(buf, axis, bit)
            lo = jnp.where(upper == 1, other, buf)
            hi = jnp.where(upper == 1, buf, other)
            buf = jnp.concatenate([lo, hi])
    return buf, results


def chunk_layer(left_tap_input, middle, right_tap_input, grad_in, conv_weight, out_weight):
    channels = middle.shape[1]
    w_low = conv_weight[:channels]
    w_mid = conv_weight[channels : 2 * channels]
    w_high = conv_weight[2 * channels :]
    preact = jnp.dot(left_tap_input, w_low, preferred_element_type=jnp.float32)
    preact = preact + jnp.dot(middle, w_mid, preferred_element_type=jnp.float32)
    preact = preact + jnp.dot(right_tap_input, w_high, preferred_element_type=jnp.float32)
    tanh_part = jnp.tanh(preact[:, :channels])
    sigm_part = jax.nn.sigmoid(preact[:, channels:])
    gated_out = (tanh_part * sigm_part).astype(jnp.bfloat16)
    first_dims = (((0,), (0,)), ((), ()))
    last_dims = (((1,), (1,)), ((), ()))
    grad_wout = lax.dot_general(gated_out, grad_in, first_dims, preferred_element_type=jnp.float32)
    grad_gated = lax.dot_general(grad_in, out_weight, last_dims, preferred_element_type=jnp.float32)
    grad_filt = grad_gated * sigm_part * (1.0 - tanh_part * tanh_part)
    grad_gate = grad_gated * tanh_part * sigm_part * (1.0 - sigm_part)
    grad_pre = jnp.concatenate([grad_filt, grad_gate], axis=1).astype(jnp.bfloat16)
    grad_wconv = jnp.concatenate(
        [
            lax.dot_general(left_tap_input, grad_pre, first_dims, preferred_element_type=jnp.float32),
            lax.dot_general(middle, grad_pre, first_dims, preferred_element_type=jnp.float32),
            lax.dot_general(right_tap_input, grad_pre, first_dims, preferred_element_type=jnp.float32),
        ],
        axis=0,
    )
    lower_term = lax.dot_general(grad_pre, w_low, last_dims, preferred_element_type=jnp.float32).astype(jnp.bfloat16)
    term_mid = lax.dot_general(grad_pre, w_mid, last_dims, preferred_element_type=jnp.float32)
    upper_term = lax.dot_general(grad_pre, w_high, last_dims, preferred_element_type=jnp.float32).astype(jnp.bfloat16)
    return grad_wconv, grad_wout, lower_term, term_mid, upper_term


def body(activations, cotangent, conv_weight, out_weight):
    positions, channels = activations.shape
    seq_size = lax.axis_size("seq")
    spacing = TAP_SPACING // positions
    rows = positions // CHUNKS
    wconv_total = None
    wout_total = None
    lows, mids, highs = [], [], []
    for k in range(CHUNKS):
        middle = activations[k * rows : (k + 1) * rows]
        grad_in = cotangent[k * rows : (k + 1) * rows]
        left_tap_input = from_behind(middle, "seq", spacing)
        right_tap_input = from_behind(middle, "seq", -spacing)
        grad_wconv, grad_wout, lower_term, term_mid, upper_term = chunk_layer(
            left_tap_input, middle, right_tap_input, grad_in, conv_weight, out_weight
        )
        wconv_total = grad_wconv if wconv_total is None else wconv_total + grad_wconv
        wout_total = grad_wout if wout_total is None else wout_total + grad_wout
        lows.append(lower_term)
        mids.append(term_mid)
        highs.append(upper_term)
    lower_all = jnp.concatenate(lows, axis=0)
    upper_all = jnp.concatenate(highs, axis=0)
    piece = positions // TERM_PIECES

    def rider(p):
        return lambda: (
            from_behind(lower_all[p * piece : (p + 1) * piece], "seq", -spacing),
            from_behind(upper_all[p * piece : (p + 1) * piece], "seq", spacing),
        )

    norm_factor = 1.0 / math.sqrt(positions * seq_size)
    flat = jnp.concatenate([wconv_total.reshape(-1), wout_total.reshape(-1)])
    summed, received = all_reduce_sum(
        flat, "seq", jnp.float32(norm_factor), [rider(p) for p in range(TERM_PIECES)]
    )
    received_ahead = jnp.concatenate([pair[0] for pair in received], axis=0)
    received_behind = jnp.concatenate([pair[1] for pair in received], axis=0)
    total_sum = cotangent.astype(jnp.float32) + jnp.concatenate(mids, axis=0)
    total_sum = total_sum + received_ahead.astype(jnp.float32) + received_behind.astype(jnp.float32)
    grad_input = total_sum.astype(jnp.bfloat16)
    split = wconv_total.size
    grad_conv = summed[:split].reshape(wconv_total.shape)
    grad_out = summed[split:].reshape(wout_total.shape)
    return grad_input, grad_conv, grad_out


def solution(mesh):
    in_specs = (P(("grp", "seq"), None), P(("grp", "seq"), None), P(), P())
    out_specs = (P(("grp", "seq"), None), P("grp", None), P("grp", None))
    return jax.shard_map(body, mesh=mesh, in_specs=in_specs, out_specs=out_specs, check_vma=False)
```

```python
import math

import jax
import jax.numpy as jnp
from jax import lax
from jax.sharding import PartitionSpec as P

TAP_SPACING = 16384
CHUNK_EIGHTHS = (2, 2, 2, 1, 1)
EARLY = 1


def from_behind(value, axis, steps):
    count = lax.axis_size(axis)
    pairs = [(source, (source + steps) % count) for source in range(count)]
    return lax.ppermute(value, axis, pairs)


def exchange(value, axis, bit):
    count = lax.axis_size(axis)
    pairs = [(source, source ^ bit) for source in range(count)]
    return lax.ppermute(value, axis, pairs)


def chain_steps(count):
    bits = []
    bit = 1
    while bit < count:
        bits.append(bit)
        bit *= 2
    return [(bit, True) for bit in bits] + [(bit, False) for bit in reversed(bits)]


def chain_step(buf, axis, bit, down):
    idx = lax.axis_index(axis)
    upper = (idx // bit) % 2
    if down:
        half = buf.shape[0] // 2
        mine = lax.dynamic_slice_in_dim(buf, upper * half, half)
        theirs = lax.dynamic_slice_in_dim(buf, (1 - upper) * half, half)
        return mine + exchange(theirs, axis, bit)
    other = exchange(buf, axis, bit)
    lo = jnp.where(upper == 1, other, buf)
    hi = jnp.where(upper == 1, buf, other)
    return jnp.concatenate([lo, hi])


def chunk_layer(left_tap_input, middle, right_tap_input, grad_in, conv_weight, out_weight):
    channels = middle.shape[1]
    w_low = conv_weight[:channels]
    w_mid = conv_weight[channels : 2 * channels]
    w_high = conv_weight[2 * channels :]
    preact = jnp.dot(left_tap_input, w_low, preferred_element_type=jnp.float32)
    preact = preact + jnp.dot(middle, w_mid, preferred_element_type=jnp.float32)
    preact = preact + jnp.dot(right_tap_input, w_high, preferred_element_type=jnp.float32)
    tanh_part = jnp.tanh(preact[:, :channels])
    sigm_part = jax.nn.sigmoid(preact[:, channels:])
    gated_out = (tanh_part * sigm_part).astype(jnp.bfloat16)
    first_dims = (((0,), (0,)), ((), ()))
    last_dims = (((1,), (1,)), ((), ()))
    grad_wout = lax.dot_general(gated_out, grad_in, first_dims, preferred_element_type=jnp.float32)
    grad_gated = lax.dot_general(grad_in, out_weight, last_dims, preferred_element_type=jnp.float32)
    grad_filt = grad_gated * sigm_part * (1.0 - tanh_part * tanh_part)
    grad_gate = grad_gated * tanh_part * sigm_part * (1.0 - sigm_part)
    grad_pre = jnp.concatenate([grad_filt, grad_gate], axis=1).astype(jnp.bfloat16)
    grad_wconv = jnp.concatenate(
        [
            lax.dot_general(left_tap_input, grad_pre, first_dims, preferred_element_type=jnp.float32),
            lax.dot_general(middle, grad_pre, first_dims, preferred_element_type=jnp.float32),
            lax.dot_general(right_tap_input, grad_pre, first_dims, preferred_element_type=jnp.float32),
        ],
        axis=0,
    )
    lower_term = lax.dot_general(grad_pre, w_low, last_dims, preferred_element_type=jnp.float32).astype(jnp.bfloat16)
    term_mid = lax.dot_general(grad_pre, w_mid, last_dims, preferred_element_type=jnp.float32)
    upper_term = lax.dot_general(grad_pre, w_high, last_dims, preferred_element_type=jnp.float32).astype(jnp.bfloat16)
    return grad_wconv, grad_wout, lower_term, term_mid, upper_term


def body(activations, cotangent, conv_weight, out_weight):
    positions, channels = activations.shape
    seq_size = lax.axis_size("seq")
    spacing = TAP_SPACING // positions
    bounds = [0]
    for eighths in CHUNK_EIGHTHS:
        bounds.append(bounds[-1] + positions * eighths // 8)
    chunks = len(CHUNK_EIGHTHS)
    wconv_total = None
    wout_total = None
    lows, mids, highs = [], [], []
    early = []
    for k in range(chunks):
        middle = activations[bounds[k] : bounds[k + 1]]
        grad_in = cotangent[bounds[k] : bounds[k + 1]]
        left_tap_input = from_behind(middle, "seq", spacing)
        right_tap_input = from_behind(middle, "seq", -spacing)
        if k == chunks - 1:
            left_tap_input, right_tap_input, lows_early, highs_early = lax.optimization_barrier(
                (left_tap_input, right_tap_input, lows[:EARLY], highs[:EARLY])
            )
            for low, high in zip(lows_early, highs_early):
                early.append((from_behind(low, "seq", -spacing), from_behind(high, "seq", spacing)))
        grad_wconv, grad_wout, lower_term, term_mid, upper_term = chunk_layer(
            left_tap_input, middle, right_tap_input, grad_in, conv_weight, out_weight
        )
        wconv_total = grad_wconv if wconv_total is None else wconv_total + grad_wconv
        wout_total = grad_wout if wout_total is None else wout_total + grad_wout
        lows.append(lower_term)
        mids.append(term_mid)
        highs.append(upper_term)
    norm_factor = 1.0 / math.sqrt(positions * seq_size)
    buf = jnp.concatenate([wconv_total.reshape(-1), wout_total.reshape(-1)])
    steps = chain_steps(seq_size)
    late = []
    sent_late = False
    for number, (bit, down) in enumerate(steps):
        if down and bit == 4:
            buf, early = lax.optimization_barrier((buf, early))
        if not down and bit == 2:
            rest_low = jnp.concatenate(lows[EARLY:], axis=0)
            rest_high = jnp.concatenate(highs[EARLY:], axis=0)
            buf, rest_low, rest_high = lax.optimization_barrier((buf, rest_low, rest_high))
            late.append((from_behind(rest_low, "seq", -spacing), from_behind(rest_high, "seq", spacing)))
            sent_late = True
        if not down and bit == 1 and late:
            buf, late = lax.optimization_barrier((buf, late))
        buf = chain_step(buf, "seq", bit, down)
        if down and number == len(steps) // 2 - 1:
            buf = buf * jnp.float32(norm_factor)
    if not steps:
        buf = buf * jnp.float32(norm_factor)
    if not sent_late:
        for low, high in zip(lows[EARLY:], highs[EARLY:]):
            late.append((from_behind(low, "seq", -spacing), from_behind(high, "seq", spacing)))
    received = early + late
    received_ahead = jnp.concatenate([pair[0] for pair in received], axis=0)
    received_behind = jnp.concatenate([pair[1] for pair in received], axis=0)
    total_sum = cotangent.astype(jnp.float32) + jnp.concatenate(mids, axis=0)
    total_sum = total_sum + received_ahead.astype(jnp.float32) + received_behind.astype(jnp.float32)
    grad_input = total_sum.astype(jnp.bfloat16)
    split = wconv_total.size
    grad_conv = buf[:split].reshape(wconv_total.shape)
    grad_out = buf[split:].reshape(wout_total.shape)
    return grad_input, grad_conv, grad_out


def solution(mesh):
    in_specs = (P(("grp", "seq"), None), P(("grp", "seq"), None), P(), P())
    out_specs = (P(("grp", "seq"), None), P("grp", None), P("grp", None))
    return jax.shard_map(body, mesh=mesh, in_specs=in_specs, out_specs=out_specs, check_vma=False)
```

```python
import math

import jax
import jax.numpy as jnp
from jax import lax
from jax.sharding import PartitionSpec as P

TAP_SPACING = 16384
CHUNK_EIGHTHS = (2, 2, 2, 1, 1)
EARLY = 1
RIDER_ROWS = 256


def from_behind(value, axis, steps):
    count = lax.axis_size(axis)
    pairs = [(source, (source + steps) % count) for source in range(count)]
    return lax.ppermute(value, axis, pairs)


def exchange(value, axis, bit):
    count = lax.axis_size(axis)
    pairs = [(source, source ^ bit) for source in range(count)]
    return lax.ppermute(value, axis, pairs)


def chain_steps(count):
    bits = []
    bit = 1
    while bit < count:
        bits.append(bit)
        bit *= 2
    return [(bit, True) for bit in bits] + [(bit, False) for bit in reversed(bits)]


def chain_step(buf, axis, bit, down):
    idx = lax.axis_index(axis)
    upper = (idx // bit) % 2
    if down:
        half = buf.shape[0] // 2
        mine = lax.dynamic_slice_in_dim(buf, upper * half, half)
        theirs = lax.dynamic_slice_in_dim(buf, (1 - upper) * half, half)
        return mine + exchange(theirs, axis, bit)
    other = exchange(buf, axis, bit)
    lo = jnp.where(upper == 1, other, buf)
    hi = jnp.where(upper == 1, buf, other)
    return jnp.concatenate([lo, hi])


def chunk_layer(left_tap_input, middle, right_tap_input, grad_in, conv_weight, out_weight):
    channels = middle.shape[1]
    w_low = conv_weight[:channels]
    w_mid = conv_weight[channels : 2 * channels]
    w_high = conv_weight[2 * channels :]
    preact = jnp.dot(left_tap_input, w_low, preferred_element_type=jnp.float32)
    preact = preact + jnp.dot(middle, w_mid, preferred_element_type=jnp.float32)
    preact = preact + jnp.dot(right_tap_input, w_high, preferred_element_type=jnp.float32)
    tanh_part = jnp.tanh(preact[:, :channels])
    sigm_part = jax.nn.sigmoid(preact[:, channels:])
    gated_out = (tanh_part * sigm_part).astype(jnp.bfloat16)
    first_dims = (((0,), (0,)), ((), ()))
    last_dims = (((1,), (1,)), ((), ()))
    grad_wout = lax.dot_general(gated_out, grad_in, first_dims, preferred_element_type=jnp.float32)
    grad_gated = lax.dot_general(grad_in, out_weight, last_dims, preferred_element_type=jnp.float32)
    grad_filt = grad_gated * sigm_part * (1.0 - tanh_part * tanh_part)
    grad_gate = grad_gated * tanh_part * sigm_part * (1.0 - sigm_part)
    grad_pre = jnp.concatenate([grad_filt, grad_gate], axis=1).astype(jnp.bfloat16)
    grad_wconv = jnp.concatenate(
        [
            lax.dot_general(left_tap_input, grad_pre, first_dims, preferred_element_type=jnp.float32),
            lax.dot_general(middle, grad_pre, first_dims, preferred_element_type=jnp.float32),
            lax.dot_general(right_tap_input, grad_pre, first_dims, preferred_element_type=jnp.float32),
        ],
        axis=0,
    )
    lower_term = lax.dot_general(grad_pre, w_low, last_dims, preferred_element_type=jnp.float32).astype(jnp.bfloat16)
    term_mid = lax.dot_general(grad_pre, w_mid, last_dims, preferred_element_type=jnp.float32)
    upper_term = lax.dot_general(grad_pre, w_high, last_dims, preferred_element_type=jnp.float32).astype(jnp.bfloat16)
    return grad_wconv, grad_wout, lower_term, term_mid, upper_term


def body(activations, cotangent, conv_weight, out_weight):
    positions, channels = activations.shape
    seq_size = lax.axis_size("seq")
    spacing = TAP_SPACING // positions
    bounds = [0]
    for eighths in CHUNK_EIGHTHS:
        bounds.append(bounds[-1] + positions * eighths // 8)
    chunks = len(CHUNK_EIGHTHS)
    wconv_total = None
    wout_total = None
    lows, mids, highs = [], [], []
    early = []
    for k in range(chunks):
        middle = activations[bounds[k] : bounds[k + 1]]
        grad_in = cotangent[bounds[k] : bounds[k + 1]]
        left_tap_input = from_behind(middle, "seq", spacing)
        right_tap_input = from_behind(middle, "seq", -spacing)
        if k == chunks - 1:
            left_tap_input, right_tap_input, lows_early, highs_early = lax.optimization_barrier(
                (left_tap_input, right_tap_input, lows[:EARLY], highs[:EARLY])
            )
            for low, high in zip(lows_early, highs_early):
                early.append((from_behind(low, "seq", -spacing), from_behind(high, "seq", spacing)))
        grad_wconv, grad_wout, lower_term, term_mid, upper_term = chunk_layer(
            left_tap_input, middle, right_tap_input, grad_in, conv_weight, out_weight
        )
        wconv_total = grad_wconv if wconv_total is None else wconv_total + grad_wconv
        wout_total = grad_wout if wout_total is None else wout_total + grad_wout
        lows.append(lower_term)
        mids.append(term_mid)
        highs.append(upper_term)
    norm_factor = 1.0 / math.sqrt(positions * seq_size)
    buf = jnp.concatenate([wconv_total.reshape(-1), wout_total.reshape(-1)])
    lower_all = jnp.concatenate(lows, axis=0)
    upper_all = jnp.concatenate(highs, axis=0)

    def send_rows(low_high, start, stop):
        return (
            from_behind(low_high[0][start:stop], "seq", -spacing),
            from_behind(low_high[1][start:stop], "seq", spacing),
        )

    steps = chain_steps(seq_size)
    rider_steps = [(4, True), (8, True), (8, False), (4, False)]
    sent_rows = bounds[EARLY]
    pending = None
    late = []
    for number, (bit, down) in enumerate(steps):
        if down and bit == 4:
            buf, early = lax.optimization_barrier((buf, early))
        if pending is not None:
            buf, pending = lax.optimization_barrier((buf, pending))
            early.append(pending)
            pending = None
        if (bit, down) in rider_steps and sent_rows + RIDER_ROWS <= positions:
            buf, pieces = lax.optimization_barrier((buf, (lower_all, upper_all)))
            pending = send_rows(pieces, sent_rows, sent_rows + RIDER_ROWS)
            sent_rows += RIDER_ROWS
        if not down and bit == 2 and not late:
            buf, pieces = lax.optimization_barrier((buf, (lower_all, upper_all)))
            late.append(send_rows(pieces, sent_rows, positions))
            sent_rows = positions
        if not down and bit == 1 and late:
            buf, late = lax.optimization_barrier((buf, late))
        buf = chain_step(buf, "seq", bit, down)
        if down and number == len(steps) // 2 - 1:
            buf = buf * jnp.float32(norm_factor)
    if not steps:
        buf = buf * jnp.float32(norm_factor)
    if pending is not None:
        early.append(pending)
    if sent_rows < positions:
        late.append(send_rows((lower_all, upper_all), sent_rows, positions))
    received = early + late
    received_ahead = jnp.concatenate([pair[0] for pair in received], axis=0)
    received_behind = jnp.concatenate([pair[1] for pair in received], axis=0)
    total_sum = cotangent.astype(jnp.float32) + jnp.concatenate(mids, axis=0)
    total_sum = total_sum + received_ahead.astype(jnp.float32) + received_behind.astype(jnp.float32)
    grad_input = total_sum.astype(jnp.bfloat16)
    split = wconv_total.size
    grad_conv = buf[:split].reshape(wconv_total.shape)
    grad_out = buf[split:].reshape(wout_total.shape)
    return grad_input, grad_conv, grad_out


def solution(mesh):
    in_specs = (P(("grp", "seq"), None), P(("grp", "seq"), None), P(), P())
    out_specs = (P(("grp", "seq"), None), P("grp", None), P("grp", None))
    return jax.shard_map(body, mesh=mesh, in_specs=in_specs, out_specs=out_specs, check_vma=False)
```

```python
import math

import jax
import jax.numpy as jnp
from jax import lax
from jax.sharding import PartitionSpec as P

TAP_SPACING = 16384
CHUNK_EIGHTHS = (2, 2, 2, 1, 1)
EARLY = 1
RIDER_ROWS = 512
RIDER_SPAN = 2


def from_behind(value, axis, steps):
    count = lax.axis_size(axis)
    pairs = [(source, (source + steps) % count) for source in range(count)]
    return lax.ppermute(value, axis, pairs)


def exchange(value, axis, bit):
    count = lax.axis_size(axis)
    pairs = [(source, source ^ bit) for source in range(count)]
    return lax.ppermute(value, axis, pairs)


def chain_steps(count):
    bits = []
    bit = 1
    while bit < count:
        bits.append(bit)
        bit *= 2
    return [(bit, True) for bit in bits] + [(bit, False) for bit in reversed(bits)]


def chain_step(buf, axis, bit, down):
    idx = lax.axis_index(axis)
    upper = (idx // bit) % 2
    if down:
        half = buf.shape[0] // 2
        mine = lax.dynamic_slice_in_dim(buf, upper * half, half)
        theirs = lax.dynamic_slice_in_dim(buf, (1 - upper) * half, half)
        return mine + exchange(theirs, axis, bit)
    other = exchange(buf, axis, bit)
    lo = jnp.where(upper == 1, other, buf)
    hi = jnp.where(upper == 1, buf, other)
    return jnp.concatenate([lo, hi])


def chunk_layer(left_tap_input, middle, right_tap_input, grad_in, conv_weight, out_weight):
    channels = middle.shape[1]
    w_low = conv_weight[:channels]
    w_mid = conv_weight[channels : 2 * channels]
    w_high = conv_weight[2 * channels :]
    preact = jnp.dot(left_tap_input, w_low, preferred_element_type=jnp.float32)
    preact = preact + jnp.dot(middle, w_mid, preferred_element_type=jnp.float32)
    preact = preact + jnp.dot(right_tap_input, w_high, preferred_element_type=jnp.float32)
    tanh_part = jnp.tanh(preact[:, :channels])
    sigm_part = jax.nn.sigmoid(preact[:, channels:])
    gated_out = (tanh_part * sigm_part).astype(jnp.bfloat16)
    first_dims = (((0,), (0,)), ((), ()))
    last_dims = (((1,), (1,)), ((), ()))
    grad_wout = lax.dot_general(gated_out, grad_in, first_dims, preferred_element_type=jnp.float32)
    grad_gated = lax.dot_general(grad_in, out_weight, last_dims, preferred_element_type=jnp.float32)
    grad_filt = grad_gated * sigm_part * (1.0 - tanh_part * tanh_part)
    grad_gate = grad_gated * tanh_part * sigm_part * (1.0 - sigm_part)
    grad_pre = jnp.concatenate([grad_filt, grad_gate], axis=1).astype(jnp.bfloat16)
    grad_wconv = jnp.concatenate(
        [
            lax.dot_general(left_tap_input, grad_pre, first_dims, preferred_element_type=jnp.float32),
            lax.dot_general(middle, grad_pre, first_dims, preferred_element_type=jnp.float32),
            lax.dot_general(right_tap_input, grad_pre, first_dims, preferred_element_type=jnp.float32),
        ],
        axis=0,
    )
    lower_term = lax.dot_general(grad_pre, w_low, last_dims, preferred_element_type=jnp.float32).astype(jnp.bfloat16)
    term_mid = lax.dot_general(grad_pre, w_mid, last_dims, preferred_element_type=jnp.float32)
    upper_term = lax.dot_general(grad_pre, w_high, last_dims, preferred_element_type=jnp.float32).astype(jnp.bfloat16)
    return grad_wconv, grad_wout, lower_term, term_mid, upper_term


def body(activations, cotangent, conv_weight, out_weight):
    positions, channels = activations.shape
    seq_size = lax.axis_size("seq")
    spacing = TAP_SPACING // positions
    bounds = [0]
    for eighths in CHUNK_EIGHTHS:
        bounds.append(bounds[-1] + positions * eighths // 8)
    chunks = len(CHUNK_EIGHTHS)
    wconv_total = None
    wout_total = None
    lows, mids, highs = [], [], []
    early = []
    for k in range(chunks):
        middle = activations[bounds[k] : bounds[k + 1]]
        grad_in = cotangent[bounds[k] : bounds[k + 1]]
        left_tap_input = from_behind(middle, "seq", spacing)
        right_tap_input = from_behind(middle, "seq", -spacing)
        if k == chunks - 1:
            left_tap_input, right_tap_input, lows_early, highs_early = lax.optimization_barrier(
                (left_tap_input, right_tap_input, lows[:EARLY], highs[:EARLY])
            )
            for low, high in zip(lows_early, highs_early):
                early.append((from_behind(low, "seq", -spacing), from_behind(high, "seq", spacing)))
        grad_wconv, grad_wout, lower_term, term_mid, upper_term = chunk_layer(
            left_tap_input, middle, right_tap_input, grad_in, conv_weight, out_weight
        )
        wconv_total = grad_wconv if wconv_total is None else wconv_total + grad_wconv
        wout_total = grad_wout if wout_total is None else wout_total + grad_wout
        lows.append(lower_term)
        mids.append(term_mid)
        highs.append(upper_term)
    norm_factor = 1.0 / math.sqrt(positions * seq_size)
    buf = jnp.concatenate([wconv_total.reshape(-1), wout_total.reshape(-1)])
    lower_all = jnp.concatenate(lows, axis=0)
    upper_all = jnp.concatenate(highs, axis=0)

    def send_rows(low_high, start, stop):
        return (
            from_behind(low_high[0][start:stop], "seq", -spacing),
            from_behind(low_high[1][start:stop], "seq", spacing),
        )

    steps = chain_steps(seq_size)
    rider_steps = [(4, True), (8, True), (8, False), (4, False)]
    sent_rows = bounds[EARLY]
    pending = []
    late = []
    for number, (bit, down) in enumerate(steps):
        if down and bit == 4:
            buf, early = lax.optimization_barrier((buf, early))
        due = [item for item in pending if item[1] <= number]
        if due:
            buf, landed = lax.optimization_barrier((buf, [item[0] for item in due]))
            early.extend(landed)
            pending = [item for item in pending if item[1] > number]
        if (bit, down) in rider_steps and sent_rows + RIDER_ROWS <= positions:
            buf, pieces = lax.optimization_barrier((buf, (lower_all, upper_all)))
            pending.append((send_rows(pieces, sent_rows, sent_rows + RIDER_ROWS), number + RIDER_SPAN))
            sent_rows += RIDER_ROWS
        if not down and bit == 2 and not late:
            buf, pieces = lax.optimization_barrier((buf, (lower_all, upper_all)))
            late.append(send_rows(pieces, sent_rows, positions))
            sent_rows = positions
        if not down and bit == 1 and late:
            buf, late = lax.optimization_barrier((buf, late))
        buf = chain_step(buf, "seq", bit, down)
        if down and number == len(steps) // 2 - 1:
            buf = buf * jnp.float32(norm_factor)
    if not steps:
        buf = buf * jnp.float32(norm_factor)
    early.extend(item[0] for item in pending)
    if sent_rows < positions:
        late.append(send_rows((lower_all, upper_all), sent_rows, positions))
    received = early + late
    received_ahead = jnp.concatenate([pair[0] for pair in received], axis=0)
    received_behind = jnp.concatenate([pair[1] for pair in received], axis=0)
    total_sum = cotangent.astype(jnp.float32) + jnp.concatenate(mids, axis=0)
    total_sum = total_sum + received_ahead.astype(jnp.float32) + received_behind.astype(jnp.float32)
    grad_input = total_sum.astype(jnp.bfloat16)
    split = wconv_total.size
    grad_conv = buf[:split].reshape(wconv_total.shape)
    grad_out = buf[split:].reshape(wout_total.shape)
    return grad_input, grad_conv, grad_out


def solution(mesh):
    in_specs = (P(("grp", "seq"), None), P(("grp", "seq"), None), P(), P())
    out_specs = (P(("grp", "seq"), None), P("grp", None), P("grp", None))
    return jax.shard_map(body, mesh=mesh, in_specs=in_specs, out_specs=out_specs, check_vma=False)
```

```python
import math

import jax
import jax.numpy as jnp
from jax import lax
from jax.sharding import PartitionSpec as P

TAP_SPACING = 16384
CHUNK_EIGHTHS = (2, 2, 2, 1, 1)
EARLY = 1
RIDER_ROWS = 512
RIDER_SPAN = 2


def from_behind(value, axis, steps):
    count = lax.axis_size(axis)
    pairs = [(source, (source + steps) % count) for source in range(count)]
    return lax.ppermute(value, axis, pairs)


def exchange(value, axis, bit):
    count = lax.axis_size(axis)
    pairs = [(source, source ^ bit) for source in range(count)]
    return lax.ppermute(value, axis, pairs)


def chain_steps(count):
    bits = []
    bit = 1
    while bit < count:
        bits.append(bit)
        bit *= 2
    return [(bit, True) for bit in bits] + [(bit, False) for bit in reversed(bits)]


def chain_step(buf, axis, bit, down):
    idx = lax.axis_index(axis)
    upper = (idx // bit) % 2
    if down:
        half = buf.shape[0] // 2
        mine = lax.dynamic_slice_in_dim(buf, upper * half, half)
        theirs = lax.dynamic_slice_in_dim(buf, (1 - upper) * half, half)
        return mine + exchange(theirs, axis, bit)
    other = exchange(buf, axis, bit)
    lo = jnp.where(upper == 1, other, buf)
    hi = jnp.where(upper == 1, buf, other)
    return jnp.concatenate([lo, hi])


def chunk_layer(left_tap_input, middle, right_tap_input, grad_in, conv_weight, out_weight):
    channels = middle.shape[1]
    w_low = conv_weight[:channels]
    w_mid = conv_weight[channels : 2 * channels]
    w_high = conv_weight[2 * channels :]
    preact = jnp.dot(left_tap_input, w_low, preferred_element_type=jnp.float32)
    preact = preact + jnp.dot(middle, w_mid, preferred_element_type=jnp.float32)
    preact = preact + jnp.dot(right_tap_input, w_high, preferred_element_type=jnp.float32)
    tanh_part = jnp.tanh(preact[:, :channels])
    sigm_part = jax.nn.sigmoid(preact[:, channels:])
    gated_out = (tanh_part * sigm_part).astype(jnp.bfloat16)
    first_dims = (((0,), (0,)), ((), ()))
    last_dims = (((1,), (1,)), ((), ()))
    grad_wout = lax.dot_general(gated_out, grad_in, first_dims, preferred_element_type=jnp.float32)
    grad_gated = lax.dot_general(grad_in, out_weight, last_dims, preferred_element_type=jnp.float32)
    grad_filt = grad_gated * sigm_part * (1.0 - tanh_part * tanh_part)
    grad_gate = grad_gated * tanh_part * sigm_part * (1.0 - sigm_part)
    grad_pre = jnp.concatenate([grad_filt, grad_gate], axis=1).astype(jnp.bfloat16)
    grad_wconv = jnp.concatenate(
        [
            lax.dot_general(left_tap_input, grad_pre, first_dims, preferred_element_type=jnp.float32),
            lax.dot_general(middle, grad_pre, first_dims, preferred_element_type=jnp.float32),
            lax.dot_general(right_tap_input, grad_pre, first_dims, preferred_element_type=jnp.float32),
        ],
        axis=0,
    )
    lower_term = lax.dot_general(grad_pre, w_low, last_dims, preferred_element_type=jnp.float32).astype(jnp.bfloat16)
    term_mid = lax.dot_general(grad_pre, w_mid, last_dims, preferred_element_type=jnp.float32)
    upper_term = lax.dot_general(grad_pre, w_high, last_dims, preferred_element_type=jnp.float32).astype(jnp.bfloat16)
    return grad_wconv, grad_wout, lower_term, term_mid, upper_term


def body(activations, cotangent, conv_weight, out_weight):
    positions, channels = activations.shape
    seq_size = lax.axis_size("seq")
    spacing = TAP_SPACING // positions
    bounds = [0]
    for eighths in CHUNK_EIGHTHS:
        bounds.append(bounds[-1] + positions * eighths // 8)
    chunks = len(CHUNK_EIGHTHS)
    wconv_total = None
    wout_total = None
    lows, mids, highs = [], [], []
    early = []
    for k in range(chunks):
        middle = activations[bounds[k] : bounds[k + 1]]
        grad_in = cotangent[bounds[k] : bounds[k + 1]]
        left_tap_input = from_behind(middle, "seq", spacing)
        right_tap_input = from_behind(middle, "seq", -spacing)
        if k == chunks - 1:
            left_tap_input, right_tap_input, lows_early, highs_early = lax.optimization_barrier(
                (left_tap_input, right_tap_input, lows[:EARLY], highs[:EARLY])
            )
            for low, high in zip(lows_early, highs_early):
                early.append((from_behind(low, "seq", -spacing), from_behind(high, "seq", spacing)))
        if wconv_total is not None:
            left_tap_input, right_tap_input, wconv_total, wout_total = lax.optimization_barrier(
                (left_tap_input, right_tap_input, wconv_total, wout_total)
            )
        grad_wconv, grad_wout, lower_term, term_mid, upper_term = chunk_layer(
            left_tap_input, middle, right_tap_input, grad_in, conv_weight, out_weight
        )
        wconv_total = grad_wconv if wconv_total is None else wconv_total + grad_wconv
        wout_total = grad_wout if wout_total is None else wout_total + grad_wout
        lows.append(lower_term)
        mids.append(term_mid)
        highs.append(upper_term)
    norm_factor = 1.0 / math.sqrt(positions * seq_size)
    buf = jnp.concatenate([wconv_total.reshape(-1), wout_total.reshape(-1)])
    lower_all = jnp.concatenate(lows, axis=0)
    upper_all = jnp.concatenate(highs, axis=0)

    def send_rows(low_high, start, stop):
        return (
            from_behind(low_high[0][start:stop], "seq", -spacing),
            from_behind(low_high[1][start:stop], "seq", spacing),
        )

    steps = chain_steps(seq_size)
    rider_steps = [(4, True), (8, True), (8, False), (4, False)]
    sent_rows = bounds[EARLY]
    pending = []
    late = []
    for number, (bit, down) in enumerate(steps):
        if down and bit == 4:
            buf, early = lax.optimization_barrier((buf, early))
        due = [item for item in pending if item[1] <= number]
        if due:
            buf, landed = lax.optimization_barrier((buf, [item[0] for item in due]))
            early.extend(landed)
            pending = [item for item in pending if item[1] > number]
        if (bit, down) in rider_steps and sent_rows + RIDER_ROWS <= positions:
            buf, pieces = lax.optimization_barrier((buf, (lower_all, upper_all)))
            pending.append((send_rows(pieces, sent_rows, sent_rows + RIDER_ROWS), number + RIDER_SPAN))
            sent_rows += RIDER_ROWS
        if not down and bit == 2 and not late:
            buf, pieces = lax.optimization_barrier((buf, (lower_all, upper_all)))
            late.append(send_rows(pieces, sent_rows, positions))
            sent_rows = positions
        if not down and bit == 1 and late:
            buf, late = lax.optimization_barrier((buf, late))
        buf = chain_step(buf, "seq", bit, down)
        if down and number == len(steps) // 2 - 1:
            buf = buf * jnp.float32(norm_factor)
    if not steps:
        buf = buf * jnp.float32(norm_factor)
    early.extend(item[0] for item in pending)
    if sent_rows < positions:
        late.append(send_rows((lower_all, upper_all), sent_rows, positions))
    received = early + late
    received_ahead = jnp.concatenate([pair[0] for pair in received], axis=0)
    received_behind = jnp.concatenate([pair[1] for pair in received], axis=0)
    total_sum = cotangent.astype(jnp.float32) + jnp.concatenate(mids, axis=0)
    total_sum = total_sum + received_ahead.astype(jnp.float32) + received_behind.astype(jnp.float32)
    grad_input = total_sum.astype(jnp.bfloat16)
    split = wconv_total.size
    grad_conv = buf[:split].reshape(wconv_total.shape)
    grad_out = buf[split:].reshape(wout_total.shape)
    return grad_input, grad_conv, grad_out


def solution(mesh):
    in_specs = (P(("grp", "seq"), None), P(("grp", "seq"), None), P(), P())
    out_specs = (P(("grp", "seq"), None), P("grp", None), P("grp", None))
    return jax.shard_map(body, mesh=mesh, in_specs=in_specs, out_specs=out_specs, check_vma=False)
```

```python
import math

import jax
import jax.numpy as jnp
from jax import lax
from jax.sharding import PartitionSpec as P

TAP_SPACING = 16384
CHUNK_EIGHTHS = (2, 2, 2, 1, 1)
EARLY = 1
RIDER_ROWS = 512
RIDER_SPAN = 2


def from_behind(value, axis, steps):
    count = lax.axis_size(axis)
    pairs = [(source, (source + steps) % count) for source in range(count)]
    return lax.ppermute(value, axis, pairs)


def exchange(value, axis, bit):
    count = lax.axis_size(axis)
    pairs = [(source, source ^ bit) for source in range(count)]
    return lax.ppermute(value, axis, pairs)


def chain_steps(count):
    bits = []
    bit = 1
    while bit < count:
        bits.append(bit)
        bit *= 2
    return [(bit, True) for bit in bits] + [(bit, False) for bit in reversed(bits)]


def chain_step(buf, axis, bit, down):
    idx = lax.axis_index(axis)
    upper = (idx // bit) % 2
    if down:
        half = buf.shape[0] // 2
        mine = lax.dynamic_slice_in_dim(buf, upper * half, half)
        theirs = lax.dynamic_slice_in_dim(buf, (1 - upper) * half, half)
        return mine + exchange(theirs, axis, bit)
    other = exchange(buf, axis, bit)
    lo = jnp.where(upper == 1, other, buf)
    hi = jnp.where(upper == 1, buf, other)
    return jnp.concatenate([lo, hi])


def chunk_layer(left_tap_input, middle, right_tap_input, grad_in, conv_weight, out_weight):
    channels = middle.shape[1]
    w_low = conv_weight[:channels]
    w_mid = conv_weight[channels : 2 * channels]
    w_high = conv_weight[2 * channels :]
    preact = jnp.dot(left_tap_input, w_low, preferred_element_type=jnp.float32)
    preact = preact + jnp.dot(middle, w_mid, preferred_element_type=jnp.float32)
    preact = preact + jnp.dot(right_tap_input, w_high, preferred_element_type=jnp.float32)
    tanh_part = jnp.tanh(preact[:, :channels])
    sigm_part = jax.nn.sigmoid(preact[:, channels:])
    gated_out = (tanh_part * sigm_part).astype(jnp.bfloat16)
    first_dims = (((0,), (0,)), ((), ()))
    last_dims = (((1,), (1,)), ((), ()))
    grad_wout = lax.dot_general(gated_out, grad_in, first_dims, preferred_element_type=jnp.float32)
    grad_gated = lax.dot_general(grad_in, out_weight, last_dims, preferred_element_type=jnp.float32)
    grad_filt = grad_gated * sigm_part * (1.0 - tanh_part * tanh_part)
    grad_gate = grad_gated * tanh_part * sigm_part * (1.0 - sigm_part)
    grad_pre = jnp.concatenate([grad_filt, grad_gate], axis=1).astype(jnp.bfloat16)
    grad_wconv = jnp.concatenate(
        [
            lax.dot_general(left_tap_input, grad_pre, first_dims, preferred_element_type=jnp.float32),
            lax.dot_general(middle, grad_pre, first_dims, preferred_element_type=jnp.float32),
            lax.dot_general(right_tap_input, grad_pre, first_dims, preferred_element_type=jnp.float32),
        ],
        axis=0,
    )
    lower_term = lax.dot_general(grad_pre, w_low, last_dims, preferred_element_type=jnp.float32).astype(jnp.bfloat16)
    term_mid = lax.dot_general(grad_pre, w_mid, last_dims, preferred_element_type=jnp.float32)
    upper_term = lax.dot_general(grad_pre, w_high, last_dims, preferred_element_type=jnp.float32).astype(jnp.bfloat16)
    return grad_wconv, grad_wout, lower_term, term_mid, upper_term


def body(activations, cotangent, conv_weight, out_weight):
    positions, channels = activations.shape
    seq_size = lax.axis_size("seq")
    spacing = TAP_SPACING // positions
    bounds = [0]
    for eighths in CHUNK_EIGHTHS:
        bounds.append(bounds[-1] + positions * eighths // 8)
    chunks = len(CHUNK_EIGHTHS)
    wconv_total = None
    wout_total = None
    lows, mids, highs = [], [], []
    early = []
    for k in range(chunks):
        middle = activations[bounds[k] : bounds[k + 1]]
        grad_in = cotangent[bounds[k] : bounds[k + 1]]
        left_tap_input = from_behind(middle, "seq", spacing)
        right_tap_input = from_behind(middle, "seq", -spacing)
        if k == chunks - 1:
            left_tap_input, right_tap_input, lows_early, highs_early = lax.optimization_barrier(
                (left_tap_input, right_tap_input, lows[:EARLY], highs[:EARLY])
            )
            for low, high in zip(lows_early, highs_early):
                half = low.shape[0] // 2
                for part in (slice(0, half), slice(half, low.shape[0])):
                    early.append((from_behind(low[part], "seq", -spacing), from_behind(high[part], "seq", spacing)))
        if wconv_total is not None:
            left_tap_input, right_tap_input, wconv_total, wout_total = lax.optimization_barrier(
                (left_tap_input, right_tap_input, wconv_total, wout_total)
            )
        grad_wconv, grad_wout, lower_term, term_mid, upper_term = chunk_layer(
            left_tap_input, middle, right_tap_input, grad_in, conv_weight, out_weight
        )
        wconv_total = grad_wconv if wconv_total is None else wconv_total + grad_wconv
        wout_total = grad_wout if wout_total is None else wout_total + grad_wout
        lows.append(lower_term)
        mids.append(term_mid)
        highs.append(upper_term)
    norm_factor = 1.0 / math.sqrt(positions * seq_size)
    buf = jnp.concatenate([wconv_total.reshape(-1), wout_total.reshape(-1)])
    lower_all = jnp.concatenate(lows, axis=0)
    upper_all = jnp.concatenate(highs, axis=0)

    def send_rows(low_high, start, stop):
        return (
            from_behind(low_high[0][start:stop], "seq", -spacing),
            from_behind(low_high[1][start:stop], "seq", spacing),
        )

    steps = chain_steps(seq_size)
    rider_steps = [(4, True), (8, True), (8, False), (4, False)]
    sent_rows = bounds[EARLY]
    pending = []
    late = []
    for number, (bit, down) in enumerate(steps):
        if down and bit == 4:
            buf, early = lax.optimization_barrier((buf, early))
        due = [item for item in pending if item[1] <= number]
        if due:
            buf, landed = lax.optimization_barrier((buf, [item[0] for item in due]))
            early.extend(landed)
            pending = [item for item in pending if item[1] > number]
        if (bit, down) in rider_steps and sent_rows + RIDER_ROWS <= positions:
            buf, pieces = lax.optimization_barrier((buf, (lower_all, upper_all)))
            pending.append((send_rows(pieces, sent_rows, sent_rows + RIDER_ROWS), number + RIDER_SPAN))
            sent_rows += RIDER_ROWS
        if not down and bit == 2 and not late:
            buf, pieces = lax.optimization_barrier((buf, (lower_all, upper_all)))
            middle_row = sent_rows + (positions - sent_rows) // 2
            late.append(send_rows(pieces, sent_rows, middle_row))
            late.append(send_rows(pieces, middle_row, positions))
            sent_rows = positions
        if not down and bit == 1 and late:
            buf, late = lax.optimization_barrier((buf, late))
        buf = chain_step(buf, "seq", bit, down)
        if down and number == len(steps) // 2 - 1:
            buf = buf * jnp.float32(norm_factor)
    if not steps:
        buf = buf * jnp.float32(norm_factor)
    early.extend(item[0] for item in pending)
    if sent_rows < positions:
        late.append(send_rows((lower_all, upper_all), sent_rows, positions))
    received = early + late
    received_ahead = jnp.concatenate([pair[0] for pair in received], axis=0)
    received_behind = jnp.concatenate([pair[1] for pair in received], axis=0)
    total_sum = cotangent.astype(jnp.float32) + jnp.concatenate(mids, axis=0)
    total_sum = total_sum + received_ahead.astype(jnp.float32) + received_behind.astype(jnp.float32)
    grad_input = total_sum.astype(jnp.bfloat16)
    split = wconv_total.size
    grad_conv = buf[:split].reshape(wconv_total.shape)
    grad_out = buf[split:].reshape(wout_total.shape)
    return grad_input, grad_conv, grad_out


def solution(mesh):
    in_specs = (P(("grp", "seq"), None), P(("grp", "seq"), None), P(), P())
    out_specs = (P(("grp", "seq"), None), P("grp", None), P("grp", None))
    return jax.shard_map(body, mesh=mesh, in_specs=in_specs, out_specs=out_specs, check_vma=False)
```

```python
import math

import jax
import jax.numpy as jnp
from jax import lax
from jax.sharding import PartitionSpec as P

TAP_SPACING = 16384
CHUNK_EIGHTHS = (2, 2, 2, 1, 1)
EARLY = 1
RIDER_ROWS = 512
RIDER_PARTS = 2
RIDER_SPAN = 1


def from_behind(value, axis, steps):
    count = lax.axis_size(axis)
    pairs = [(source, (source + steps) % count) for source in range(count)]
    return lax.ppermute(value, axis, pairs)


def exchange(value, axis, bit):
    count = lax.axis_size(axis)
    pairs = [(source, source ^ bit) for source in range(count)]
    return lax.ppermute(value, axis, pairs)


def chain_steps(count):
    bits = []
    bit = 1
    while bit < count:
        bits.append(bit)
        bit *= 2
    return [(bit, True) for bit in bits] + [(bit, False) for bit in reversed(bits)]


def chain_step(buf, axis, bit, down):
    idx = lax.axis_index(axis)
    upper = (idx // bit) % 2
    if down:
        half = buf.shape[0] // 2
        mine = lax.dynamic_slice_in_dim(buf, upper * half, half)
        theirs = lax.dynamic_slice_in_dim(buf, (1 - upper) * half, half)
        return mine + exchange(theirs, axis, bit)
    other = exchange(buf, axis, bit)
    lo = jnp.where(upper == 1, other, buf)
    hi = jnp.where(upper == 1, buf, other)
    return jnp.concatenate([lo, hi])


def chunk_layer(left_tap_input, middle, right_tap_input, grad_in, conv_weight, out_weight):
    channels = middle.shape[1]
    w_low = conv_weight[:channels]
    w_mid = conv_weight[channels : 2 * channels]
    w_high = conv_weight[2 * channels :]
    preact = jnp.dot(left_tap_input, w_low, preferred_element_type=jnp.float32)
    preact = preact + jnp.dot(middle, w_mid, preferred_element_type=jnp.float32)
    preact = preact + jnp.dot(right_tap_input, w_high, preferred_element_type=jnp.float32)
    tanh_part = jnp.tanh(preact[:, :channels])
    sigm_part = jax.nn.sigmoid(preact[:, channels:])
    gated_out = (tanh_part * sigm_part).astype(jnp.bfloat16)
    first_dims = (((0,), (0,)), ((), ()))
    last_dims = (((1,), (1,)), ((), ()))
    grad_wout = lax.dot_general(gated_out, grad_in, first_dims, preferred_element_type=jnp.float32)
    grad_gated = lax.dot_general(grad_in, out_weight, last_dims, preferred_element_type=jnp.float32)
    grad_filt = grad_gated * sigm_part * (1.0 - tanh_part * tanh_part)
    grad_gate = grad_gated * tanh_part * sigm_part * (1.0 - sigm_part)
    grad_pre = jnp.concatenate([grad_filt, grad_gate], axis=1).astype(jnp.bfloat16)
    grad_wconv = jnp.concatenate(
        [
            lax.dot_general(left_tap_input, grad_pre, first_dims, preferred_element_type=jnp.float32),
            lax.dot_general(middle, grad_pre, first_dims, preferred_element_type=jnp.float32),
            lax.dot_general(right_tap_input, grad_pre, first_dims, preferred_element_type=jnp.float32),
        ],
        axis=0,
    )
    lower_term = lax.dot_general(grad_pre, w_low, last_dims, preferred_element_type=jnp.float32).astype(jnp.bfloat16)
    term_mid = lax.dot_general(grad_pre, w_mid, last_dims, preferred_element_type=jnp.float32)
    upper_term = lax.dot_general(grad_pre, w_high, last_dims, preferred_element_type=jnp.float32).astype(jnp.bfloat16)
    return grad_wconv, grad_wout, lower_term, term_mid, upper_term


def body(activations, cotangent, conv_weight, out_weight):
    positions, channels = activations.shape
    seq_size = lax.axis_size("seq")
    spacing = TAP_SPACING // positions
    bounds = [0]
    for eighths in CHUNK_EIGHTHS:
        bounds.append(bounds[-1] + positions * eighths // 8)
    chunks = len(CHUNK_EIGHTHS)
    wconv_total = None
    wout_total = None
    lows, mids, highs = [], [], []
    early = []
    for k in range(chunks):
        middle = activations[bounds[k] : bounds[k + 1]]
        grad_in = cotangent[bounds[k] : bounds[k + 1]]
        left_tap_input = from_behind(middle, "seq", spacing)
        right_tap_input = from_behind(middle, "seq", -spacing)
        if k == chunks - 1:
            left_tap_input, right_tap_input, lows_early, highs_early = lax.optimization_barrier(
                (left_tap_input, right_tap_input, lows[:EARLY], highs[:EARLY])
            )
            for low, high in zip(lows_early, highs_early):
                half = low.shape[0] // 2
                for part in (slice(0, half), slice(half, low.shape[0])):
                    early.append((from_behind(low[part], "seq", -spacing), from_behind(high[part], "seq", spacing)))
        if wconv_total is not None:
            left_tap_input, right_tap_input, wconv_total, wout_total = lax.optimization_barrier(
                (left_tap_input, right_tap_input, wconv_total, wout_total)
            )
        grad_wconv, grad_wout, lower_term, term_mid, upper_term = chunk_layer(
            left_tap_input, middle, right_tap_input, grad_in, conv_weight, out_weight
        )
        wconv_total = grad_wconv if wconv_total is None else wconv_total + grad_wconv
        wout_total = grad_wout if wout_total is None else wout_total + grad_wout
        lows.append(lower_term)
        mids.append(term_mid)
        highs.append(upper_term)
    norm_factor = 1.0 / math.sqrt(positions * seq_size)
    buf = jnp.concatenate([wconv_total.reshape(-1), wout_total.reshape(-1)])
    lower_all = jnp.concatenate(lows, axis=0)
    upper_all = jnp.concatenate(highs, axis=0)

    def send_rows(low_high, start, stop):
        return (
            from_behind(low_high[0][start:stop], "seq", -spacing),
            from_behind(low_high[1][start:stop], "seq", spacing),
        )

    steps = chain_steps(seq_size)
    rider_steps = [(4, True), (8, True), (8, False), (4, False)]
    sent_rows = bounds[EARLY]
    pending = []
    late = []
    for number, (bit, down) in enumerate(steps):
        if down and bit == 4:
            buf, early = lax.optimization_barrier((buf, early))
        due = [item for item in pending if item[1] <= number]
        if due:
            buf, landed = lax.optimization_barrier((buf, [item[0] for item in due]))
            early.extend(landed)
            pending = [item for item in pending if item[1] > number]
        if (bit, down) in rider_steps and sent_rows + RIDER_ROWS <= positions:
            buf, pieces = lax.optimization_barrier((buf, (lower_all, upper_all)))
            for part in range(RIDER_PARTS):
                start = sent_rows + part * RIDER_ROWS // RIDER_PARTS
                stop = sent_rows + (part + 1) * RIDER_ROWS // RIDER_PARTS
                pending.append((send_rows(pieces, start, stop), number + RIDER_SPAN))
            sent_rows += RIDER_ROWS
        if not down and bit == 2 and not late:
            buf, pieces = lax.optimization_barrier((buf, (lower_all, upper_all)))
            middle_row = sent_rows + (positions - sent_rows) // 2
            late.append(send_rows(pieces, sent_rows, middle_row))
            late.append(send_rows(pieces, middle_row, positions))
            sent_rows = positions
        if not down and bit == 1 and late:
            buf, late = lax.optimization_barrier((buf, late))
        buf = chain_step(buf, "seq", bit, down)
        if down and number == len(steps) // 2 - 1:
            buf = buf * jnp.float32(norm_factor)
    if not steps:
        buf = buf * jnp.float32(norm_factor)
    early.extend(item[0] for item in pending)
    if sent_rows < positions:
        late.append(send_rows((lower_all, upper_all), sent_rows, positions))
    received = early + late
    received_ahead = jnp.concatenate([pair[0] for pair in received], axis=0)
    received_behind = jnp.concatenate([pair[1] for pair in received], axis=0)
    total_sum = cotangent.astype(jnp.float32) + jnp.concatenate(mids, axis=0)
    total_sum = total_sum + received_ahead.astype(jnp.float32) + received_behind.astype(jnp.float32)
    grad_input = total_sum.astype(jnp.bfloat16)
    split = wconv_total.size
    grad_conv = buf[:split].reshape(wconv_total.shape)
    grad_out = buf[split:].reshape(wout_total.shape)
    return grad_input, grad_conv, grad_out


def solution(mesh):
    in_specs = (P(("grp", "seq"), None), P(("grp", "seq"), None), P(), P())
    out_specs = (P(("grp", "seq"), None), P("grp", None), P("grp", None))
    return jax.shard_map(body, mesh=mesh, in_specs=in_specs, out_specs=out_specs, check_vma=False)
```

```python
import math

import jax
import jax.numpy as jnp
from jax import lax
from jax.sharding import PartitionSpec as P

TAP_SPACING = 16384
CHUNK_EIGHTHS = (2, 2, 2, 1, 1)
EARLY = 1
RIDER_ROWS = 512
RIDER_SPAN = 2


def from_behind(value, axis, steps):
    count = lax.axis_size(axis)
    pairs = [(source, (source + steps) % count) for source in range(count)]
    return lax.ppermute(value, axis, pairs)


def exchange(value, axis, bit):
    count = lax.axis_size(axis)
    pairs = [(source, source ^ bit) for source in range(count)]
    return lax.ppermute(value, axis, pairs)


def chain_steps(count):
    bits = []
    bit = 1
    while bit < count:
        bits.append(bit)
        bit *= 2
    return [(bit, True) for bit in bits] + [(bit, False) for bit in reversed(bits)]


def chain_step(buf, axis, bit, down):
    idx = lax.axis_index(axis)
    upper = (idx // bit) % 2
    if down:
        half = buf.shape[0] // 2
        mine = lax.dynamic_slice_in_dim(buf, upper * half, half)
        theirs = lax.dynamic_slice_in_dim(buf, (1 - upper) * half, half)
        return mine + exchange(theirs, axis, bit)
    other = exchange(buf, axis, bit)
    lo = jnp.where(upper == 1, other, buf)
    hi = jnp.where(upper == 1, buf, other)
    return jnp.concatenate([lo, hi])


def chunk_layer(left_tap_input, middle, right_tap_input, grad_in, conv_weight, out_weight):
    channels = middle.shape[1]
    w_low = conv_weight[:channels]
    w_mid = conv_weight[channels : 2 * channels]
    w_high = conv_weight[2 * channels :]
    preact = jnp.dot(left_tap_input, w_low, preferred_element_type=jnp.float32)
    preact = preact + jnp.dot(middle, w_mid, preferred_element_type=jnp.float32)
    preact = preact + jnp.dot(right_tap_input, w_high, preferred_element_type=jnp.float32)
    tanh_part = jnp.tanh(preact[:, :channels])
    sigm_part = jax.nn.sigmoid(preact[:, channels:])
    gated_out = (tanh_part * sigm_part).astype(jnp.bfloat16)
    first_dims = (((0,), (0,)), ((), ()))
    last_dims = (((1,), (1,)), ((), ()))
    grad_wout = lax.dot_general(gated_out, grad_in, first_dims, preferred_element_type=jnp.float32)
    grad_gated = lax.dot_general(grad_in, out_weight, last_dims, preferred_element_type=jnp.float32)
    grad_filt = grad_gated * sigm_part * (1.0 - tanh_part * tanh_part)
    grad_gate = grad_gated * tanh_part * sigm_part * (1.0 - sigm_part)
    grad_pre = jnp.concatenate([grad_filt, grad_gate], axis=1).astype(jnp.bfloat16)
    grad_wconv = jnp.concatenate(
        [
            lax.dot_general(left_tap_input, grad_pre, first_dims, preferred_element_type=jnp.float32),
            lax.dot_general(middle, grad_pre, first_dims, preferred_element_type=jnp.float32),
            lax.dot_general(right_tap_input, grad_pre, first_dims, preferred_element_type=jnp.float32),
        ],
        axis=0,
    )
    lower_term = lax.dot_general(grad_pre, w_low, last_dims, preferred_element_type=jnp.float32).astype(jnp.bfloat16)
    term_mid = lax.dot_general(grad_pre, w_mid, last_dims, preferred_element_type=jnp.float32)
    upper_term = lax.dot_general(grad_pre, w_high, last_dims, preferred_element_type=jnp.float32).astype(jnp.bfloat16)
    return grad_wconv, grad_wout, lower_term, term_mid, upper_term


def body(activations, cotangent, conv_weight, out_weight):
    positions, channels = activations.shape
    seq_size = lax.axis_size("seq")
    spacing = TAP_SPACING // positions
    bounds = [0]
    for eighths in CHUNK_EIGHTHS:
        bounds.append(bounds[-1] + positions * eighths // 8)
    chunks = len(CHUNK_EIGHTHS)
    wconv_total = None
    wout_total = None
    lows, mids, highs = [], [], []
    early = []
    for k in range(chunks):
        middle = activations[bounds[k] : bounds[k + 1]]
        grad_in = cotangent[bounds[k] : bounds[k + 1]]
        left_tap_input = from_behind(middle, "seq", spacing)
        right_tap_input = from_behind(middle, "seq", -spacing)
        if k == chunks - 1:
            left_tap_input, right_tap_input, lows_early, highs_early = lax.optimization_barrier(
                (left_tap_input, right_tap_input, lows[:EARLY], highs[:EARLY])
            )
            for low, high in zip(lows_early, highs_early):
                half = low.shape[0] // 2
                for part in (slice(0, half), slice(half, low.shape[0])):
                    early.append((from_behind(low[part], "seq", -spacing), from_behind(high[part], "seq", spacing)))
        if wconv_total is not None:
            left_tap_input, right_tap_input, wconv_total, wout_total = lax.optimization_barrier(
                (left_tap_input, right_tap_input, wconv_total, wout_total)
            )
        grad_wconv, grad_wout, lower_term, term_mid, upper_term = chunk_layer(
            left_tap_input, middle, right_tap_input, grad_in, conv_weight, out_weight
        )
        wconv_total = grad_wconv if wconv_total is None else wconv_total + grad_wconv
        wout_total = grad_wout if wout_total is None else wout_total + grad_wout
        lows.append(lower_term)
        mids.append(term_mid)
        highs.append(upper_term)
    norm_factor = 1.0 / math.sqrt(positions * seq_size)
    wout_rows = wout_total.reshape(-1, wconv_total.shape[1])
    buf = jnp.concatenate([wconv_total, wout_rows], axis=0)
    lower_all = jnp.concatenate(lows, axis=0)
    upper_all = jnp.concatenate(highs, axis=0)

    def send_rows(low_high, start, stop):
        return (
            from_behind(low_high[0][start:stop], "seq", -spacing),
            from_behind(low_high[1][start:stop], "seq", spacing),
        )

    steps = chain_steps(seq_size)
    rider_steps = [(4, True), (8, True), (8, False), (4, False)]
    sent_rows = bounds[EARLY]
    pending = []
    late = []
    for number, (bit, down) in enumerate(steps):
        if down and bit == 4:
            buf, early = lax.optimization_barrier((buf, early))
        due = [item for item in pending if item[1] <= number]
        if due:
            buf, landed = lax.optimization_barrier((buf, [item[0] for item in due]))
            early.extend(landed)
            pending = [item for item in pending if item[1] > number]
        if (bit, down) in rider_steps and sent_rows + RIDER_ROWS <= positions:
            buf, pieces = lax.optimization_barrier((buf, (lower_all, upper_all)))
            pending.append((send_rows(pieces, sent_rows, sent_rows + RIDER_ROWS), number + RIDER_SPAN))
            sent_rows += RIDER_ROWS
        if not down and bit == 2 and not late:
            buf, pieces = lax.optimization_barrier((buf, (lower_all, upper_all)))
            middle_row = sent_rows + (positions - sent_rows) // 2
            late.append(send_rows(pieces, sent_rows, middle_row))
            late.append(send_rows(pieces, middle_row, positions))
            sent_rows = positions
        if not down and bit == 1 and late:
            buf, late = lax.optimization_barrier((buf, late))
        buf = chain_step(buf, "seq", bit, down)
        if down and number == len(steps) // 2 - 1:
            buf = buf * jnp.float32(norm_factor)
    if not steps:
        buf = buf * jnp.float32(norm_factor)
    early.extend(item[0] for item in pending)
    if sent_rows < positions:
        late.append(send_rows((lower_all, upper_all), sent_rows, positions))
    received = early + late
    received_ahead = jnp.concatenate([pair[0] for pair in received], axis=0)
    received_behind = jnp.concatenate([pair[1] for pair in received], axis=0)
    total_sum = cotangent.astype(jnp.float32) + jnp.concatenate(mids, axis=0)
    total_sum = total_sum + received_ahead.astype(jnp.float32) + received_behind.astype(jnp.float32)
    grad_input = total_sum.astype(jnp.bfloat16)
    split = wconv_total.shape[0]
    grad_conv = buf[:split]
    grad_out = buf[split:].reshape(wout_total.shape)
    return grad_input, grad_conv, grad_out


def solution(mesh):
    in_specs = (P(("grp", "seq"), None), P(("grp", "seq"), None), P(), P())
    out_specs = (P(("grp", "seq"), None), P("grp", None), P("grp", None))
    return jax.shard_map(body, mesh=mesh, in_specs=in_specs, out_specs=out_specs, check_vma=False)
```

```python
import math

import jax
import jax.numpy as jnp
from jax import lax
from jax.sharding import PartitionSpec as P

TAP_SPACING = 16384
CHUNK_EIGHTHS = (2, 2, 2, 1, 1)
EARLY = 1
RIDER_ROWS = 512
RIDER_SPAN = 2
LATE_BIT = 4


def from_behind(value, axis, steps):
    count = lax.axis_size(axis)
    pairs = [(source, (source + steps) % count) for source in range(count)]
    return lax.ppermute(value, axis, pairs)


def exchange(value, axis, bit):
    count = lax.axis_size(axis)
    pairs = [(source, source ^ bit) for source in range(count)]
    return lax.ppermute(value, axis, pairs)


def chain_steps(count):
    bits = []
    bit = 1
    while bit < count:
        bits.append(bit)
        bit *= 2
    return [(bit, True) for bit in bits] + [(bit, False) for bit in reversed(bits)]


def chain_step(buf, axis, bit, down):
    idx = lax.axis_index(axis)
    upper = (idx // bit) % 2
    if down:
        half = buf.shape[0] // 2
        mine = lax.dynamic_slice_in_dim(buf, upper * half, half)
        theirs = lax.dynamic_slice_in_dim(buf, (1 - upper) * half, half)
        return mine + exchange(theirs, axis, bit)
    other = exchange(buf, axis, bit)
    lo = jnp.where(upper == 1, other, buf)
    hi = jnp.where(upper == 1, buf, other)
    return jnp.concatenate([lo, hi])


def chunk_layer(left_tap_input, middle, right_tap_input, grad_in, conv_weight, out_weight):
    channels = middle.shape[1]
    w_low = conv_weight[:channels]
    w_mid = conv_weight[channels : 2 * channels]
    w_high = conv_weight[2 * channels :]
    preact = jnp.dot(left_tap_input, w_low, preferred_element_type=jnp.float32)
    preact = preact + jnp.dot(middle, w_mid, preferred_element_type=jnp.float32)
    preact = preact + jnp.dot(right_tap_input, w_high, preferred_element_type=jnp.float32)
    tanh_part = jnp.tanh(preact[:, :channels])
    sigm_part = jax.nn.sigmoid(preact[:, channels:])
    gated_out = (tanh_part * sigm_part).astype(jnp.bfloat16)
    first_dims = (((0,), (0,)), ((), ()))
    last_dims = (((1,), (1,)), ((), ()))
    grad_wout = lax.dot_general(gated_out, grad_in, first_dims, preferred_element_type=jnp.float32)
    grad_gated = lax.dot_general(grad_in, out_weight, last_dims, preferred_element_type=jnp.float32)
    grad_filt = grad_gated * sigm_part * (1.0 - tanh_part * tanh_part)
    grad_gate = grad_gated * tanh_part * sigm_part * (1.0 - sigm_part)
    grad_pre = jnp.concatenate([grad_filt, grad_gate], axis=1).astype(jnp.bfloat16)
    grad_wconv = jnp.concatenate(
        [
            lax.dot_general(left_tap_input, grad_pre, first_dims, preferred_element_type=jnp.float32),
            lax.dot_general(middle, grad_pre, first_dims, preferred_element_type=jnp.float32),
            lax.dot_general(right_tap_input, grad_pre, first_dims, preferred_element_type=jnp.float32),
        ],
        axis=0,
    )
    lower_term = lax.dot_general(grad_pre, w_low, last_dims, preferred_element_type=jnp.float32).astype(jnp.bfloat16)
    term_mid = lax.dot_general(grad_pre, w_mid, last_dims, preferred_element_type=jnp.float32)
    upper_term = lax.dot_general(grad_pre, w_high, last_dims, preferred_element_type=jnp.float32).astype(jnp.bfloat16)
    return grad_wconv, grad_wout, lower_term, term_mid, upper_term


def body(activations, cotangent, conv_weight, out_weight):
    positions, channels = activations.shape
    seq_size = lax.axis_size("seq")
    spacing = TAP_SPACING // positions
    bounds = [0]
    for eighths in CHUNK_EIGHTHS:
        bounds.append(bounds[-1] + positions * eighths // 8)
    chunks = len(CHUNK_EIGHTHS)
    wconv_total = None
    wout_total = None
    lows, mids, highs = [], [], []
    early = []
    for k in range(chunks):
        middle = activations[bounds[k] : bounds[k + 1]]
        grad_in = cotangent[bounds[k] : bounds[k + 1]]
        left_tap_input = from_behind(middle, "seq", spacing)
        right_tap_input = from_behind(middle, "seq", -spacing)
        if k == chunks - 1:
            left_tap_input, right_tap_input, lows_early, highs_early = lax.optimization_barrier(
                (left_tap_input, right_tap_input, lows[:EARLY], highs[:EARLY])
            )
            for low, high in zip(lows_early, highs_early):
                half = low.shape[0] // 2
                for part in (slice(0, half), slice(half, low.shape[0])):
                    early.append((from_behind(low[part], "seq", -spacing), from_behind(high[part], "seq", spacing)))
        if wconv_total is not None:
            left_tap_input, right_tap_input, wconv_total, wout_total = lax.optimization_barrier(
                (left_tap_input, right_tap_input, wconv_total, wout_total)
            )
        grad_wconv, grad_wout, lower_term, term_mid, upper_term = chunk_layer(
            left_tap_input, middle, right_tap_input, grad_in, conv_weight, out_weight
        )
        wconv_total = grad_wconv if wconv_total is None else wconv_total + grad_wconv
        wout_total = grad_wout if wout_total is None else wout_total + grad_wout
        lows.append(lower_term)
        mids.append(term_mid)
        highs.append(upper_term)
    norm_factor = 1.0 / math.sqrt(positions * seq_size)
    wout_rows = wout_total.reshape(-1, wconv_total.shape[1])
    buf = jnp.concatenate([wconv_total, wout_rows], axis=0)
    lower_all = jnp.concatenate(lows, axis=0)
    upper_all = jnp.concatenate(highs, axis=0)

    def send_rows(low_high, start, stop):
        return (
            from_behind(low_high[0][start:stop], "seq", -spacing),
            from_behind(low_high[1][start:stop], "seq", spacing),
        )

    steps = chain_steps(seq_size)
    rider_steps = [(4, True), (8, True), (8, False), (4, False)]
    sent_rows = bounds[EARLY]
    pending = []
    late = []
    for number, (bit, down) in enumerate(steps):
        if down and bit == 4:
            buf, early = lax.optimization_barrier((buf, early))
        due = [item for item in pending if item[1] <= number]
        if due:
            buf, landed = lax.optimization_barrier((buf, [item[0] for item in due]))
            early.extend(landed)
            pending = [item for item in pending if item[1] > number]
        if (bit, down) in rider_steps and sent_rows + RIDER_ROWS <= positions:
            buf, pieces = lax.optimization_barrier((buf, (lower_all, upper_all)))
            pending.append((send_rows(pieces, sent_rows, sent_rows + RIDER_ROWS), number + RIDER_SPAN))
            sent_rows += RIDER_ROWS
        if not down and bit == LATE_BIT and not late:
            buf, pieces = lax.optimization_barrier((buf, (lower_all, upper_all)))
            middle_row = sent_rows + (positions - sent_rows) // 2
            late.append(send_rows(pieces, sent_rows, middle_row))
            late.append(send_rows(pieces, middle_row, positions))
            sent_rows = positions
        if not down and bit == 1 and late:
            buf, late = lax.optimization_barrier((buf, late))
        buf = chain_step(buf, "seq", bit, down)
        if down and number == len(steps) // 2 - 1:
            buf = buf * jnp.float32(norm_factor)
    if not steps:
        buf = buf * jnp.float32(norm_factor)
    early.extend(item[0] for item in pending)
    if sent_rows < positions:
        late.append(send_rows((lower_all, upper_all), sent_rows, positions))
    received = early + late
    received_ahead = jnp.concatenate([pair[0] for pair in received], axis=0)
    received_behind = jnp.concatenate([pair[1] for pair in received], axis=0)
    total_sum = cotangent.astype(jnp.float32) + jnp.concatenate(mids, axis=0)
    total_sum = total_sum + received_ahead.astype(jnp.float32) + received_behind.astype(jnp.float32)
    grad_input = total_sum.astype(jnp.bfloat16)
    split = wconv_total.shape[0]
    grad_conv = buf[:split]
    grad_out = buf[split:].reshape(wout_total.shape)
    return grad_input, grad_conv, grad_out


def solution(mesh):
    in_specs = (P(("grp", "seq"), None), P(("grp", "seq"), None), P(), P())
    out_specs = (P(("grp", "seq"), None), P("grp", None), P("grp", None))
    return jax.shard_map(body, mesh=mesh, in_specs=in_specs, out_specs=out_specs, check_vma=False)
```

```python
import math

import jax
import jax.numpy as jnp
from jax import lax
from jax.sharding import PartitionSpec as P

TAP_SPACING = 16384
CHUNK_EIGHTHS = (2, 2, 2, 1, 1)
EARLY = 1
RIDER_ROWS = 512
RIDER_SPAN = 2


def from_behind(value, axis, steps):
    count = lax.axis_size(axis)
    pairs = [(source, (source + steps) % count) for source in range(count)]
    return lax.ppermute(value, axis, pairs)


def exchange(value, axis, bit):
    count = lax.axis_size(axis)
    pairs = [(source, source ^ bit) for source in range(count)]
    return lax.ppermute(value, axis, pairs)


def chain_steps(count):
    bits = []
    bit = 1
    while bit < count:
        bits.append(bit)
        bit *= 2
    return [(bit, True) for bit in bits] + [(bit, False) for bit in reversed(bits)]


def chain_step(buf, axis, bit, down):
    idx = lax.axis_index(axis)
    upper = (idx // bit) % 2
    if down:
        half = buf.shape[0] // 2
        mine = lax.dynamic_slice_in_dim(buf, upper * half, half)
        theirs = lax.dynamic_slice_in_dim(buf, (1 - upper) * half, half)
        return mine + exchange(theirs, axis, bit)
    other = exchange(buf, axis, bit)
    lo = jnp.where(upper == 1, other, buf)
    hi = jnp.where(upper == 1, buf, other)
    return jnp.concatenate([lo, hi])


def chunk_layer(left_tap_input, middle, right_tap_input, grad_in, conv_weight, out_weight):
    channels = middle.shape[1]
    w_low = conv_weight[:channels]
    w_mid = conv_weight[channels : 2 * channels]
    w_high = conv_weight[2 * channels :]
    preact = jnp.dot(left_tap_input, w_low, preferred_element_type=jnp.float32)
    preact = preact + jnp.dot(middle, w_mid, preferred_element_type=jnp.float32)
    preact = preact + jnp.dot(right_tap_input, w_high, preferred_element_type=jnp.float32)
    tanh_part = jnp.tanh(preact[:, :channels])
    sigm_part = jax.nn.sigmoid(preact[:, channels:])
    gated_out = (tanh_part * sigm_part).astype(jnp.bfloat16)
    first_dims = (((0,), (0,)), ((), ()))
    last_dims = (((1,), (1,)), ((), ()))
    grad_wout = lax.dot_general(gated_out, grad_in, first_dims, preferred_element_type=jnp.float32)
    grad_gated = lax.dot_general(grad_in, out_weight, last_dims, preferred_element_type=jnp.float32)
    grad_filt = grad_gated * sigm_part * (1.0 - tanh_part * tanh_part)
    grad_gate = grad_gated * tanh_part * sigm_part * (1.0 - sigm_part)
    grad_pre = jnp.concatenate([grad_filt, grad_gate], axis=1).astype(jnp.bfloat16)
    grad_wconv = jnp.concatenate(
        [
            lax.dot_general(left_tap_input, grad_pre, first_dims, preferred_element_type=jnp.float32),
            lax.dot_general(middle, grad_pre, first_dims, preferred_element_type=jnp.float32),
            lax.dot_general(right_tap_input, grad_pre, first_dims, preferred_element_type=jnp.float32),
        ],
        axis=0,
    )
    lower_term = lax.dot_general(grad_pre, w_low, last_dims, preferred_element_type=jnp.float32).astype(jnp.bfloat16)
    term_mid = lax.dot_general(grad_pre, w_mid, last_dims, preferred_element_type=jnp.float32)
    upper_term = lax.dot_general(grad_pre, w_high, last_dims, preferred_element_type=jnp.float32).astype(jnp.bfloat16)
    return grad_wconv, grad_wout, lower_term, term_mid, upper_term


def body(activations, cotangent, conv_weight, out_weight):
    positions, channels = activations.shape
    seq_size = lax.axis_size("seq")
    spacing = TAP_SPACING // positions
    bounds = [0]
    for eighths in CHUNK_EIGHTHS:
        bounds.append(bounds[-1] + positions * eighths // 8)
    chunks = len(CHUNK_EIGHTHS)
    wconv_total = None
    wout_total = None
    lows, mids, highs = [], [], []
    early = []
    for k in range(chunks):
        middle = activations[bounds[k] : bounds[k + 1]]
        grad_in = cotangent[bounds[k] : bounds[k + 1]]
        left_tap_input = from_behind(middle, "seq", spacing)
        right_tap_input = from_behind(middle, "seq", -spacing)
        if k == chunks - 1:
            left_tap_input, right_tap_input, lows_early, highs_early = lax.optimization_barrier(
                (left_tap_input, right_tap_input, lows[:EARLY], highs[:EARLY])
            )
            for low, high in zip(lows_early, highs_early):
                half = low.shape[0] // 2
                for part in (slice(0, half), slice(half, low.shape[0])):
                    early.append((from_behind(low[part], "seq", -spacing), from_behind(high[part], "seq", spacing)))
        if wconv_total is not None:
            left_tap_input, right_tap_input, wconv_total, wout_total = lax.optimization_barrier(
                (left_tap_input, right_tap_input, wconv_total, wout_total)
            )
        grad_wconv, grad_wout, lower_term, term_mid, upper_term = chunk_layer(
            left_tap_input, middle, right_tap_input, grad_in, conv_weight, out_weight
        )
        wconv_total = grad_wconv if wconv_total is None else wconv_total + grad_wconv
        wout_total = grad_wout if wout_total is None else wout_total + grad_wout
        lows.append(lower_term)
        mids.append(term_mid)
        highs.append(upper_term)
    norm_factor = 1.0 / math.sqrt(positions * seq_size)
    buf = jnp.concatenate([wconv_total.reshape(-1), wout_total.reshape(-1)])
    lower_all = jnp.concatenate(lows, axis=0)
    upper_all = jnp.concatenate(highs, axis=0)

    def send_rows(low_high, start, stop):
        return (
            from_behind(low_high[0][start:stop], "seq", -spacing),
            from_behind(low_high[1][start:stop], "seq", spacing),
        )

    steps = chain_steps(seq_size)
    rider_steps = [(4, True), (8, True), (8, False), (4, False)]
    sent_rows = bounds[EARLY]
    pending = []
    late = []
    for number, (bit, down) in enumerate(steps):
        if down and bit == 4:
            buf, early = lax.optimization_barrier((buf, early))
        due = [item for item in pending if item[1] <= number]
        if due:
            buf, landed = lax.optimization_barrier((buf, [item[0] for item in due]))
            early.extend(landed)
            pending = [item for item in pending if item[1] > number]
        if (bit, down) in rider_steps and sent_rows + RIDER_ROWS <= positions:
            buf, pieces = lax.optimization_barrier((buf, (lower_all, upper_all)))
            pending.append((send_rows(pieces, sent_rows, sent_rows + RIDER_ROWS), number + RIDER_SPAN))
            sent_rows += RIDER_ROWS
        if not down and bit == 2 and not late:
            buf, pieces = lax.optimization_barrier((buf, (lower_all, upper_all)))
            middle_row = sent_rows + (positions - sent_rows) // 2
            late.append(send_rows(pieces, sent_rows, middle_row))
            late.append(send_rows(pieces, middle_row, positions))
            sent_rows = positions
        if not down and bit == 1 and late:
            buf, late = lax.optimization_barrier((buf, late))
        buf = chain_step(buf, "seq", bit, down)
        if down and number == len(steps) // 2 - 1:
            buf = (buf * jnp.float32(norm_factor)).reshape(-1, wconv_total.shape[1])
    if not steps:
        buf = (buf * jnp.float32(norm_factor)).reshape(-1, wconv_total.shape[1])
    early.extend(item[0] for item in pending)
    if sent_rows < positions:
        late.append(send_rows((lower_all, upper_all), sent_rows, positions))
    received = early + late
    received_ahead = jnp.concatenate([pair[0] for pair in received], axis=0)
    received_behind = jnp.concatenate([pair[1] for pair in received], axis=0)
    total_sum = cotangent.astype(jnp.float32) + jnp.concatenate(mids, axis=0)
    total_sum = total_sum + received_ahead.astype(jnp.float32) + received_behind.astype(jnp.float32)
    grad_input = total_sum.astype(jnp.bfloat16)
    split = wconv_total.shape[0]
    grad_conv = buf[:split]
    grad_out = buf[split:].reshape(wout_total.shape)
    return grad_input, grad_conv, grad_out


def solution(mesh):
    in_specs = (P(("grp", "seq"), None), P(("grp", "seq"), None), P(), P())
    out_specs = (P(("grp", "seq"), None), P("grp", None), P("grp", None))
    return jax.shard_map(body, mesh=mesh, in_specs=in_specs, out_specs=out_specs, check_vma=False)
```

```python
import math

import jax
import jax.numpy as jnp
from jax import lax
from jax.sharding import PartitionSpec as P

TAP_SPACING = 16384
CHUNK_EIGHTHS = (2, 2, 2, 1, 1)
EARLY = 1
RIDER_ROWS = 512
RIDER_SPAN = 2


def from_behind(value, axis, steps):
    count = lax.axis_size(axis)
    pairs = [(source, (source + steps) % count) for source in range(count)]
    return lax.ppermute(value, axis, pairs)


def exchange(value, axis, bit):
    count = lax.axis_size(axis)
    pairs = [(source, source ^ bit) for source in range(count)]
    return lax.ppermute(value, axis, pairs)


def chain_steps(count):
    bits = []
    bit = 1
    while bit < count:
        bits.append(bit)
        bit *= 2
    return [(bit, True) for bit in bits] + [(bit, False) for bit in reversed(bits)]


def chain_step(buf, axis, bit, down):
    idx = lax.axis_index(axis)
    upper = (idx // bit) % 2
    if down:
        half = buf.shape[0] // 2
        mine = lax.dynamic_slice_in_dim(buf, upper * half, half)
        theirs = lax.dynamic_slice_in_dim(buf, (1 - upper) * half, half)
        return mine + exchange(theirs, axis, bit)
    other = exchange(buf, axis, bit)
    lo = jnp.where(upper == 1, other, buf)
    hi = jnp.where(upper == 1, buf, other)
    return jnp.concatenate([lo, hi])


def chunk_layer(left_tap_input, middle, right_tap_input, grad_in, conv_weight, out_weight):
    channels = middle.shape[1]
    w_low = conv_weight[:channels]
    w_mid = conv_weight[channels : 2 * channels]
    w_high = conv_weight[2 * channels :]
    preact = jnp.dot(left_tap_input, w_low, preferred_element_type=jnp.float32)
    preact = preact + jnp.dot(middle, w_mid, preferred_element_type=jnp.float32)
    preact = preact + jnp.dot(right_tap_input, w_high, preferred_element_type=jnp.float32)
    tanh_part = jnp.tanh(preact[:, :channels])
    sigm_part = jax.nn.sigmoid(preact[:, channels:])
    gated_out = (tanh_part * sigm_part).astype(jnp.bfloat16)
    first_dims = (((0,), (0,)), ((), ()))
    last_dims = (((1,), (1,)), ((), ()))
    grad_wout = lax.dot_general(gated_out, grad_in, first_dims, preferred_element_type=jnp.float32)
    grad_gated = lax.dot_general(grad_in, out_weight, last_dims, preferred_element_type=jnp.float32)
    grad_filt = grad_gated * sigm_part * (1.0 - tanh_part * tanh_part)
    grad_gate = grad_gated * tanh_part * sigm_part * (1.0 - sigm_part)
    grad_pre = jnp.concatenate([grad_filt, grad_gate], axis=1).astype(jnp.bfloat16)
    grad_wconv = jnp.concatenate(
        [
            lax.dot_general(left_tap_input, grad_pre, first_dims, preferred_element_type=jnp.float32),
            lax.dot_general(middle, grad_pre, first_dims, preferred_element_type=jnp.float32),
            lax.dot_general(right_tap_input, grad_pre, first_dims, preferred_element_type=jnp.float32),
        ],
        axis=0,
    )
    lower_term = lax.dot_general(grad_pre, w_low, last_dims, preferred_element_type=jnp.float32).astype(jnp.bfloat16)
    term_mid = lax.dot_general(grad_pre, w_mid, last_dims, preferred_element_type=jnp.float32)
    upper_term = lax.dot_general(grad_pre, w_high, last_dims, preferred_element_type=jnp.float32).astype(jnp.bfloat16)
    return grad_wconv, grad_wout, lower_term, term_mid, upper_term


def body(activations, cotangent, conv_weight, out_weight):
    positions, channels = activations.shape
    seq_size = lax.axis_size("seq")
    spacing = TAP_SPACING // positions
    bounds = [0]
    for eighths in CHUNK_EIGHTHS:
        bounds.append(bounds[-1] + positions * eighths // 8)
    chunks = len(CHUNK_EIGHTHS)
    wconv_total = None
    wout_total = None
    lows, mids, highs = [], [], []
    early = []
    for k in range(chunks):
        middle = activations[bounds[k] : bounds[k + 1]]
        grad_in = cotangent[bounds[k] : bounds[k + 1]]
        left_tap_input = from_behind(middle, "seq", spacing)
        right_tap_input = from_behind(middle, "seq", -spacing)
        if k == chunks - 1:
            left_tap_input, right_tap_input, lows_early, highs_early = lax.optimization_barrier(
                (left_tap_input, right_tap_input, lows[:EARLY], highs[:EARLY])
            )
            for low, high in zip(lows_early, highs_early):
                half = low.shape[0] // 2
                for part in (slice(0, half), slice(half, low.shape[0])):
                    early.append((from_behind(low[part], "seq", -spacing), from_behind(high[part], "seq", spacing)))
        if wconv_total is not None:
            left_tap_input, right_tap_input, wconv_total, wout_total = lax.optimization_barrier(
                (left_tap_input, right_tap_input, wconv_total, wout_total)
            )
        grad_wconv, grad_wout, lower_term, term_mid, upper_term = chunk_layer(
            left_tap_input, middle, right_tap_input, grad_in, conv_weight, out_weight
        )
        wconv_total = grad_wconv if wconv_total is None else wconv_total + grad_wconv
        wout_total = grad_wout if wout_total is None else wout_total + grad_wout
        lows.append(lower_term)
        mids.append(term_mid)
        highs.append(upper_term)
    norm_factor = 1.0 / math.sqrt(positions * seq_size)
    buf = jnp.concatenate([wconv_total.reshape(-1), wout_total.reshape(-1)])
    lower_all = jnp.concatenate(lows, axis=0)
    upper_all = jnp.concatenate(highs, axis=0)

    def send_rows(low_high, start, stop):
        return (
            from_behind(low_high[0][start:stop], "seq", -spacing),
            from_behind(low_high[1][start:stop], "seq", spacing),
        )

    steps = chain_steps(seq_size)
    rider_steps = [(4, True), (8, True), (8, False), (4, False)]
    sent_rows = bounds[EARLY]
    pending = []
    late = []
    for number, (bit, down) in enumerate(steps):
        if down and bit == 4:
            buf, early = lax.optimization_barrier((buf, early))
        due = [item for item in pending if item[1] <= number]
        if due:
            buf, landed = lax.optimization_barrier((buf, [item[0] for item in due]))
            early.extend(landed)
            pending = [item for item in pending if item[1] > number]
        if (bit, down) in rider_steps and sent_rows + RIDER_ROWS <= positions:
            buf, pieces = lax.optimization_barrier((buf, (lower_all, upper_all)))
            pending.append((send_rows(pieces, sent_rows, sent_rows + RIDER_ROWS), number + RIDER_SPAN))
            sent_rows += RIDER_ROWS
        if not down and bit == 2 and not late:
            buf, pieces = lax.optimization_barrier((buf, (lower_all, upper_all)))
            middle_row = sent_rows + (positions - sent_rows) // 2
            late.append(send_rows(pieces, sent_rows, middle_row))
            late.append(send_rows(pieces, middle_row, positions))
            sent_rows = positions
        if not down and bit == 1 and late:
            buf, late = lax.optimization_barrier((buf, late))
        buf = chain_step(buf, "seq", bit, down)
        if down and number == len(steps) // 2 - 1:
            buf = (buf * jnp.float32(norm_factor)).reshape(-1, wconv_total.shape[1])
    if not steps:
        buf = (buf * jnp.float32(norm_factor)).reshape(-1, wconv_total.shape[1])
    early.extend(item[0] for item in pending)
    if sent_rows < positions:
        late.append(send_rows((lower_all, upper_all), sent_rows, positions))
    mids_all = jnp.concatenate(mids, axis=0)

    def finish(pieces, start):
        ahead = jnp.concatenate([pair[0] for pair in pieces], axis=0)
        behind = jnp.concatenate([pair[1] for pair in pieces], axis=0)
        stop = start + ahead.shape[0]
        total_sum = cotangent[start:stop].astype(jnp.float32) + mids_all[start:stop]
        total_sum = total_sum + ahead.astype(jnp.float32) + behind.astype(jnp.float32)
        return total_sum.astype(jnp.bfloat16)

    head = finish(early, 0)
    grad_input = jnp.concatenate([head, finish(late, head.shape[0])], axis=0) if late else head
    split = wconv_total.shape[0]
    grad_conv = buf[:split]
    grad_out = buf[split:].reshape(wout_total.shape)
    return grad_input, grad_conv, grad_out


def solution(mesh):
    in_specs = (P(("grp", "seq"), None), P(("grp", "seq"), None), P(), P())
    out_specs = (P(("grp", "seq"), None), P("grp", None), P("grp", None))
    return jax.shard_map(body, mesh=mesh, in_specs=in_specs, out_specs=out_specs, check_vma=False)
```

```python
import math

import jax
import jax.numpy as jnp
from jax import lax
from jax.sharding import PartitionSpec as P

TAP_SPACING = 16384
CHUNK_EIGHTHS = (2, 2, 2, 1, 1)
EARLY = 1
RIDER_ROWS = 640
RIDER_SPAN = 2


def from_behind(value, axis, steps):
    count = lax.axis_size(axis)
    pairs = [(source, (source + steps) % count) for source in range(count)]
    return lax.ppermute(value, axis, pairs)


def exchange(value, axis, bit):
    count = lax.axis_size(axis)
    pairs = [(source, source ^ bit) for source in range(count)]
    return lax.ppermute(value, axis, pairs)


def chain_steps(count):
    bits = []
    bit = 1
    while bit < count:
        bits.append(bit)
        bit *= 2
    return [(bit, True) for bit in bits] + [(bit, False) for bit in reversed(bits)]


def chain_step(buf, axis, bit, down):
    idx = lax.axis_index(axis)
    upper = (idx // bit) % 2
    if down:
        half = buf.shape[0] // 2
        mine = lax.dynamic_slice_in_dim(buf, upper * half, half)
        theirs = lax.dynamic_slice_in_dim(buf, (1 - upper) * half, half)
        return mine + exchange(theirs, axis, bit)
    other = exchange(buf, axis, bit)
    lo = jnp.where(upper == 1, other, buf)
    hi = jnp.where(upper == 1, buf, other)
    return jnp.concatenate([lo, hi])


def chunk_layer(left_tap_input, middle, right_tap_input, grad_in, conv_weight, out_weight):
    channels = middle.shape[1]
    w_low = conv_weight[:channels]
    w_mid = conv_weight[channels : 2 * channels]
    w_high = conv_weight[2 * channels :]
    preact = jnp.dot(left_tap_input, w_low, preferred_element_type=jnp.float32)
    preact = preact + jnp.dot(middle, w_mid, preferred_element_type=jnp.float32)
    preact = preact + jnp.dot(right_tap_input, w_high, preferred_element_type=jnp.float32)
    tanh_part = jnp.tanh(preact[:, :channels])
    sigm_part = jax.nn.sigmoid(preact[:, channels:])
    gated_out = (tanh_part * sigm_part).astype(jnp.bfloat16)
    first_dims = (((0,), (0,)), ((), ()))
    last_dims = (((1,), (1,)), ((), ()))
    grad_wout = lax.dot_general(gated_out, grad_in, first_dims, preferred_element_type=jnp.float32)
    grad_gated = lax.dot_general(grad_in, out_weight, last_dims, preferred_element_type=jnp.float32)
    grad_filt = grad_gated * sigm_part * (1.0 - tanh_part * tanh_part)
    grad_gate = grad_gated * tanh_part * sigm_part * (1.0 - sigm_part)
    grad_pre = jnp.concatenate([grad_filt, grad_gate], axis=1).astype(jnp.bfloat16)
    grad_wconv = jnp.concatenate(
        [
            lax.dot_general(left_tap_input, grad_pre, first_dims, preferred_element_type=jnp.float32),
            lax.dot_general(middle, grad_pre, first_dims, preferred_element_type=jnp.float32),
            lax.dot_general(right_tap_input, grad_pre, first_dims, preferred_element_type=jnp.float32),
        ],
        axis=0,
    )
    lower_term = lax.dot_general(grad_pre, w_low, last_dims, preferred_element_type=jnp.float32).astype(jnp.bfloat16)
    term_mid = lax.dot_general(grad_pre, w_mid, last_dims, preferred_element_type=jnp.float32)
    upper_term = lax.dot_general(grad_pre, w_high, last_dims, preferred_element_type=jnp.float32).astype(jnp.bfloat16)
    return grad_wconv, grad_wout, lower_term, term_mid, upper_term


def body(activations, cotangent, conv_weight, out_weight):
    positions, channels = activations.shape
    seq_size = lax.axis_size("seq")
    spacing = TAP_SPACING // positions
    bounds = [0]
    for eighths in CHUNK_EIGHTHS:
        bounds.append(bounds[-1] + positions * eighths // 8)
    chunks = len(CHUNK_EIGHTHS)
    wconv_total = None
    wout_total = None
    lows, mids, highs = [], [], []
    early = []
    for k in range(chunks):
        middle = activations[bounds[k] : bounds[k + 1]]
        grad_in = cotangent[bounds[k] : bounds[k + 1]]
        left_tap_input = from_behind(middle, "seq", spacing)
        right_tap_input = from_behind(middle, "seq", -spacing)
        if k == chunks - 1:
            left_tap_input, right_tap_input, lows_early, highs_early = lax.optimization_barrier(
                (left_tap_input, right_tap_input, lows[:EARLY], highs[:EARLY])
            )
            for low, high in zip(lows_early, highs_early):
                half = low.shape[0] // 2
                for part in (slice(0, half), slice(half, low.shape[0])):
                    early.append((from_behind(low[part], "seq", -spacing), from_behind(high[part], "seq", spacing)))
        if wconv_total is not None:
            left_tap_input, right_tap_input, wconv_total, wout_total = lax.optimization_barrier(
                (left_tap_input, right_tap_input, wconv_total, wout_total)
            )
        grad_wconv, grad_wout, lower_term, term_mid, upper_term = chunk_layer(
            left_tap_input, middle, right_tap_input, grad_in, conv_weight, out_weight
        )
        wconv_total = grad_wconv if wconv_total is None else wconv_total + grad_wconv
        wout_total = grad_wout if wout_total is None else wout_total + grad_wout
        lows.append(lower_term)
        mids.append(term_mid)
        highs.append(upper_term)
    norm_factor = 1.0 / math.sqrt(positions * seq_size)
    buf = jnp.concatenate([wconv_total.reshape(-1), wout_total.reshape(-1)])
    lower_all = jnp.concatenate(lows, axis=0)
    upper_all = jnp.concatenate(highs, axis=0)

    def send_rows(low_high, start, stop):
        return (
            from_behind(low_high[0][start:stop], "seq", -spacing),
            from_behind(low_high[1][start:stop], "seq", spacing),
        )

    steps = chain_steps(seq_size)
    rider_steps = [(4, True), (8, True), (8, False), (4, False)]
    sent_rows = bounds[EARLY]
    pending = []
    late = []
    for number, (bit, down) in enumerate(steps):
        if down and bit == 4:
            buf, early = lax.optimization_barrier((buf, early))
        due = [item for item in pending if item[1] <= number]
        if due:
            buf, landed = lax.optimization_barrier((buf, [item[0] for item in due]))
            early.extend(landed)
            pending = [item for item in pending if item[1] > number]
        if (bit, down) in rider_steps and sent_rows + RIDER_ROWS <= positions:
            buf, pieces = lax.optimization_barrier((buf, (lower_all, upper_all)))
            pending.append((send_rows(pieces, sent_rows, sent_rows + RIDER_ROWS), number + RIDER_SPAN))
            sent_rows += RIDER_ROWS
        if not down and bit == 2 and not late:
            buf, pieces = lax.optimization_barrier((buf, (lower_all, upper_all)))
            middle_row = sent_rows + (positions - sent_rows) // 2
            late.append(send_rows(pieces, sent_rows, middle_row))
            late.append(send_rows(pieces, middle_row, positions))
            sent_rows = positions
        if not down and bit == 1 and late:
            buf, late = lax.optimization_barrier((buf, late))
        buf = chain_step(buf, "seq", bit, down)
        if down and number == len(steps) // 2 - 1:
            buf = (buf * jnp.float32(norm_factor)).reshape(-1, wconv_total.shape[1])
    if not steps:
        buf = (buf * jnp.float32(norm_factor)).reshape(-1, wconv_total.shape[1])
    early.extend(item[0] for item in pending)
    if sent_rows < positions:
        late.append(send_rows((lower_all, upper_all), sent_rows, positions))
    received = early + late
    received_ahead = jnp.concatenate([pair[0] for pair in received], axis=0)
    received_behind = jnp.concatenate([pair[1] for pair in received], axis=0)
    total_sum = cotangent.astype(jnp.float32) + jnp.concatenate(mids, axis=0)
    total_sum = total_sum + received_ahead.astype(jnp.float32) + received_behind.astype(jnp.float32)
    grad_input = total_sum.astype(jnp.bfloat16)
    split = wconv_total.shape[0]
    grad_conv = buf[:split]
    grad_out = buf[split:].reshape(wout_total.shape)
    return grad_input, grad_conv, grad_out


def solution(mesh):
    in_specs = (P(("grp", "seq"), None), P(("grp", "seq"), None), P(), P())
    out_specs = (P(("grp", "seq"), None), P("grp", None), P("grp", None))
    return jax.shard_map(body, mesh=mesh, in_specs=in_specs, out_specs=out_specs, check_vma=False)
```

```python
import math

import jax
import jax.numpy as jnp
from jax import lax
from jax.sharding import PartitionSpec as P

TAP_SPACING = 16384
CHUNK_EIGHTHS = (2, 2, 2, 2)
EARLY = 1
RIDER_ROWS = 512
RIDER_SPAN = 2


def from_behind(value, axis, steps):
    count = lax.axis_size(axis)
    pairs = [(source, (source + steps) % count) for source in range(count)]
    return lax.ppermute(value, axis, pairs)


def exchange(value, axis, bit):
    count = lax.axis_size(axis)
    pairs = [(source, source ^ bit) for source in range(count)]
    return lax.ppermute(value, axis, pairs)


def chain_steps(count):
    bits = []
    bit = 1
    while bit < count:
        bits.append(bit)
        bit *= 2
    return [(bit, True) for bit in bits] + [(bit, False) for bit in reversed(bits)]


def chain_step(buf, axis, bit, down):
    idx = lax.axis_index(axis)
    upper = (idx // bit) % 2
    if down:
        half = buf.shape[0] // 2
        mine = lax.dynamic_slice_in_dim(buf, upper * half, half)
        theirs = lax.dynamic_slice_in_dim(buf, (1 - upper) * half, half)
        return mine + exchange(theirs, axis, bit)
    other = exchange(buf, axis, bit)
    lo = jnp.where(upper == 1, other, buf)
    hi = jnp.where(upper == 1, buf, other)
    return jnp.concatenate([lo, hi])


def chunk_layer(left_tap_input, middle, right_tap_input, grad_in, conv_weight, out_weight):
    channels = middle.shape[1]
    w_low = conv_weight[:channels]
    w_mid = conv_weight[channels : 2 * channels]
    w_high = conv_weight[2 * channels :]
    preact = jnp.dot(left_tap_input, w_low, preferred_element_type=jnp.float32)
    preact = preact + jnp.dot(middle, w_mid, preferred_element_type=jnp.float32)
    preact = preact + jnp.dot(right_tap_input, w_high, preferred_element_type=jnp.float32)
    tanh_part = jnp.tanh(preact[:, :channels])
    sigm_part = jax.nn.sigmoid(preact[:, channels:])
    gated_out = (tanh_part * sigm_part).astype(jnp.bfloat16)
    first_dims = (((0,), (0,)), ((), ()))
    last_dims = (((1,), (1,)), ((), ()))
    grad_wout = lax.dot_general(gated_out, grad_in, first_dims, preferred_element_type=jnp.float32)
    grad_gated = lax.dot_general(grad_in, out_weight, last_dims, preferred_element_type=jnp.float32)
    grad_filt = grad_gated * sigm_part * (1.0 - tanh_part * tanh_part)
    grad_gate = grad_gated * tanh_part * sigm_part * (1.0 - sigm_part)
    grad_pre = jnp.concatenate([grad_filt, grad_gate], axis=1).astype(jnp.bfloat16)
    grad_wconv = jnp.concatenate(
        [
            lax.dot_general(left_tap_input, grad_pre, first_dims, preferred_element_type=jnp.float32),
            lax.dot_general(middle, grad_pre, first_dims, preferred_element_type=jnp.float32),
            lax.dot_general(right_tap_input, grad_pre, first_dims, preferred_element_type=jnp.float32),
        ],
        axis=0,
    )
    lower_term = lax.dot_general(grad_pre, w_low, last_dims, preferred_element_type=jnp.float32).astype(jnp.bfloat16)
    term_mid = lax.dot_general(grad_pre, w_mid, last_dims, preferred_element_type=jnp.float32)
    upper_term = lax.dot_general(grad_pre, w_high, last_dims, preferred_element_type=jnp.float32).astype(jnp.bfloat16)
    return grad_wconv, grad_wout, lower_term, term_mid, upper_term


def body(activations, cotangent, conv_weight, out_weight):
    positions, channels = activations.shape
    seq_size = lax.axis_size("seq")
    spacing = TAP_SPACING // positions
    bounds = [0]
    for eighths in CHUNK_EIGHTHS:
        bounds.append(bounds[-1] + positions * eighths // 8)
    chunks = len(CHUNK_EIGHTHS)
    wconv_total = None
    wout_total = None
    lows, mids, highs = [], [], []
    early = []
    for k in range(chunks):
        middle = activations[bounds[k] : bounds[k + 1]]
        grad_in = cotangent[bounds[k] : bounds[k + 1]]
        left_tap_input = from_behind(middle, "seq", spacing)
        right_tap_input = from_behind(middle, "seq", -spacing)
        if k == chunks - 1:
            left_tap_input, right_tap_input, lows_early, highs_early = lax.optimization_barrier(
                (left_tap_input, right_tap_input, lows[:EARLY], highs[:EARLY])
            )
            for low, high in zip(lows_early, highs_early):
                half = low.shape[0] // 2
                for part in (slice(0, half), slice(half, low.shape[0])):
                    early.append((from_behind(low[part], "seq", -spacing), from_behind(high[part], "seq", spacing)))
        if wconv_total is not None:
            left_tap_input, right_tap_input, wconv_total, wout_total = lax.optimization_barrier(
                (left_tap_input, right_tap_input, wconv_total, wout_total)
            )
        grad_wconv, grad_wout, lower_term, term_mid, upper_term = chunk_layer(
            left_tap_input, middle, right_tap_input, grad_in, conv_weight, out_weight
        )
        wconv_total = grad_wconv if wconv_total is None else wconv_total + grad_wconv
        wout_total = grad_wout if wout_total is None else wout_total + grad_wout
        lows.append(lower_term)
        mids.append(term_mid)
        highs.append(upper_term)
    norm_factor = 1.0 / math.sqrt(positions * seq_size)
    buf = jnp.concatenate([wconv_total.reshape(-1), wout_total.reshape(-1)])
    lower_all = jnp.concatenate(lows, axis=0)
    upper_all = jnp.concatenate(highs, axis=0)

    def send_rows(low_high, start, stop):
        return (
            from_behind(low_high[0][start:stop], "seq", -spacing),
            from_behind(low_high[1][start:stop], "seq", spacing),
        )

    steps = chain_steps(seq_size)
    rider_steps = [(4, True), (8, True), (8, False), (4, False)]
    sent_rows = bounds[EARLY]
    pending = []
    late = []
    for number, (bit, down) in enumerate(steps):
        if down and bit == 4:
            buf, early = lax.optimization_barrier((buf, early))
        due = [item for item in pending if item[1] <= number]
        if due:
            buf, landed = lax.optimization_barrier((buf, [item[0] for item in due]))
            early.extend(landed)
            pending = [item for item in pending if item[1] > number]
        if (bit, down) in rider_steps and sent_rows + RIDER_ROWS <= positions:
            buf, pieces = lax.optimization_barrier((buf, (lower_all, upper_all)))
            pending.append((send_rows(pieces, sent_rows, sent_rows + RIDER_ROWS), number + RIDER_SPAN))
            sent_rows += RIDER_ROWS
        if not down and bit == 2 and not late:
            buf, pieces = lax.optimization_barrier((buf, (lower_all, upper_all)))
            middle_row = sent_rows + (positions - sent_rows) // 2
            late.append(send_rows(pieces, sent_rows, middle_row))
            late.append(send_rows(pieces, middle_row, positions))
            sent_rows = positions
        if not down and bit == 1 and late:
            buf, late = lax.optimization_barrier((buf, late))
        buf = chain_step(buf, "seq", bit, down)
        if down and number == len(steps) // 2 - 1:
            buf = (buf * jnp.float32(norm_factor)).reshape(-1, wconv_total.shape[1])
    if not steps:
        buf = (buf * jnp.float32(norm_factor)).reshape(-1, wconv_total.shape[1])
    early.extend(item[0] for item in pending)
    if sent_rows < positions:
        late.append(send_rows((lower_all, upper_all), sent_rows, positions))
    received = early + late
    received_ahead = jnp.concatenate([pair[0] for pair in received], axis=0)
    received_behind = jnp.concatenate([pair[1] for pair in received], axis=0)
    total_sum = cotangent.astype(jnp.float32) + jnp.concatenate(mids, axis=0)
    total_sum = total_sum + received_ahead.astype(jnp.float32) + received_behind.astype(jnp.float32)
    grad_input = total_sum.astype(jnp.bfloat16)
    split = wconv_total.shape[0]
    grad_conv = buf[:split]
    grad_out = buf[split:].reshape(wout_total.shape)
    return grad_input, grad_conv, grad_out


def solution(mesh):
    in_specs = (P(("grp", "seq"), None), P(("grp", "seq"), None), P(), P())
    out_specs = (P(("grp", "seq"), None), P("grp", None), P("grp", None))
    return jax.shard_map(body, mesh=mesh, in_specs=in_specs, out_specs=out_specs, check_vma=False)
```

```python
import math

import jax
import jax.numpy as jnp
from jax import lax
from jax.sharding import PartitionSpec as P

TAP_SPACING = 16384
CHUNK_SIXTEENTHS = (4, 4, 4, 2, 1, 1)
EARLY = 1
RIDER_ROWS = 512
RIDER_SPAN = 2


def from_behind(value, axis, steps):
    count = lax.axis_size(axis)
    pairs = [(source, (source + steps) % count) for source in range(count)]
    return lax.ppermute(value, axis, pairs)


def exchange(value, axis, bit):
    count = lax.axis_size(axis)
    pairs = [(source, source ^ bit) for source in range(count)]
    return lax.ppermute(value, axis, pairs)


def chain_steps(count):
    bits = []
    bit = 1
    while bit < count:
        bits.append(bit)
        bit *= 2
    return [(bit, True) for bit in bits] + [(bit, False) for bit in reversed(bits)]


def chain_step(buf, axis, bit, down):
    idx = lax.axis_index(axis)
    upper = (idx // bit) % 2
    if down:
        half = buf.shape[0] // 2
        mine = lax.dynamic_slice_in_dim(buf, upper * half, half)
        theirs = lax.dynamic_slice_in_dim(buf, (1 - upper) * half, half)
        return mine + exchange(theirs, axis, bit)
    other = exchange(buf, axis, bit)
    lo = jnp.where(upper == 1, other, buf)
    hi = jnp.where(upper == 1, buf, other)
    return jnp.concatenate([lo, hi])


def chunk_layer(left_tap_input, middle, right_tap_input, grad_in, conv_weight, out_weight):
    channels = middle.shape[1]
    w_low = conv_weight[:channels]
    w_mid = conv_weight[channels : 2 * channels]
    w_high = conv_weight[2 * channels :]
    preact = jnp.dot(left_tap_input, w_low, preferred_element_type=jnp.float32)
    preact = preact + jnp.dot(middle, w_mid, preferred_element_type=jnp.float32)
    preact = preact + jnp.dot(right_tap_input, w_high, preferred_element_type=jnp.float32)
    tanh_part = jnp.tanh(preact[:, :channels])
    sigm_part = jax.nn.sigmoid(preact[:, channels:])
    gated_out = (tanh_part * sigm_part).astype(jnp.bfloat16)
    first_dims = (((0,), (0,)), ((), ()))
    last_dims = (((1,), (1,)), ((), ()))
    grad_wout = lax.dot_general(gated_out, grad_in, first_dims, preferred_element_type=jnp.float32)
    grad_gated = lax.dot_general(grad_in, out_weight, last_dims, preferred_element_type=jnp.float32)
    grad_filt = grad_gated * sigm_part * (1.0 - tanh_part * tanh_part)
    grad_gate = grad_gated * tanh_part * sigm_part * (1.0 - sigm_part)
    grad_pre = jnp.concatenate([grad_filt, grad_gate], axis=1).astype(jnp.bfloat16)
    grad_wconv = jnp.concatenate(
        [
            lax.dot_general(left_tap_input, grad_pre, first_dims, preferred_element_type=jnp.float32),
            lax.dot_general(middle, grad_pre, first_dims, preferred_element_type=jnp.float32),
            lax.dot_general(right_tap_input, grad_pre, first_dims, preferred_element_type=jnp.float32),
        ],
        axis=0,
    )
    lower_term = lax.dot_general(grad_pre, w_low, last_dims, preferred_element_type=jnp.float32).astype(jnp.bfloat16)
    term_mid = lax.dot_general(grad_pre, w_mid, last_dims, preferred_element_type=jnp.float32)
    upper_term = lax.dot_general(grad_pre, w_high, last_dims, preferred_element_type=jnp.float32).astype(jnp.bfloat16)
    return grad_wconv, grad_wout, lower_term, term_mid, upper_term


def body(activations, cotangent, conv_weight, out_weight):
    positions, channels = activations.shape
    seq_size = lax.axis_size("seq")
    spacing = TAP_SPACING // positions
    bounds = [0]
    for sixteenths in CHUNK_SIXTEENTHS:
        bounds.append(bounds[-1] + positions * sixteenths // 16)
    chunks = len(CHUNK_SIXTEENTHS)
    wconv_total = None
    wout_total = None
    lows, mids, highs = [], [], []
    early = []
    for k in range(chunks):
        middle = activations[bounds[k] : bounds[k + 1]]
        grad_in = cotangent[bounds[k] : bounds[k + 1]]
        left_tap_input = from_behind(middle, "seq", spacing)
        right_tap_input = from_behind(middle, "seq", -spacing)
        if k == chunks - 1:
            left_tap_input, right_tap_input, lows_early, highs_early = lax.optimization_barrier(
                (left_tap_input, right_tap_input, lows[:EARLY], highs[:EARLY])
            )
            for low, high in zip(lows_early, highs_early):
                half = low.shape[0] // 2
                for part in (slice(0, half), slice(half, low.shape[0])):
                    early.append((from_behind(low[part], "seq", -spacing), from_behind(high[part], "seq", spacing)))
        if wconv_total is not None:
            left_tap_input, right_tap_input, wconv_total, wout_total = lax.optimization_barrier(
                (left_tap_input, right_tap_input, wconv_total, wout_total)
            )
        grad_wconv, grad_wout, lower_term, term_mid, upper_term = chunk_layer(
            left_tap_input, middle, right_tap_input, grad_in, conv_weight, out_weight
        )
        wconv_total = grad_wconv if wconv_total is None else wconv_total + grad_wconv
        wout_total = grad_wout if wout_total is None else wout_total + grad_wout
        lows.append(lower_term)
        mids.append(term_mid)
        highs.append(upper_term)
    norm_factor = 1.0 / math.sqrt(positions * seq_size)
    buf = jnp.concatenate([wconv_total.reshape(-1), wout_total.reshape(-1)])
    lower_all = jnp.concatenate(lows, axis=0)
    upper_all = jnp.concatenate(highs, axis=0)

    def send_rows(low_high, start, stop):
        return (
            from_behind(low_high[0][start:stop], "seq", -spacing),
            from_behind(low_high[1][start:stop], "seq", spacing),
        )

    steps = chain_steps(seq_size)
    rider_steps = [(4, True), (8, True), (8, False), (4, False)]
    sent_rows = bounds[EARLY]
    pending = []
    late = []
    for number, (bit, down) in enumerate(steps):
        if down and bit == 4:
            buf, early = lax.optimization_barrier((buf, early))
        due = [item for item in pending if item[1] <= number]
        if due:
            buf, landed = lax.optimization_barrier((buf, [item[0] for item in due]))
            early.extend(landed)
            pending = [item for item in pending if item[1] > number]
        if (bit, down) in rider_steps and sent_rows + RIDER_ROWS <= positions:
            buf, pieces = lax.optimization_barrier((buf, (lower_all, upper_all)))
            pending.append((send_rows(pieces, sent_rows, sent_rows + RIDER_ROWS), number + RIDER_SPAN))
            sent_rows += RIDER_ROWS
        if not down and bit == 2 and not late:
            buf, pieces = lax.optimization_barrier((buf, (lower_all, upper_all)))
            middle_row = sent_rows + (positions - sent_rows) // 2
            late.append(send_rows(pieces, sent_rows, middle_row))
            late.append(send_rows(pieces, middle_row, positions))
            sent_rows = positions
        if not down and bit == 1 and late:
            buf, late = lax.optimization_barrier((buf, late))
        buf = chain_step(buf, "seq", bit, down)
        if down and number == len(steps) // 2 - 1:
            buf = (buf * jnp.float32(norm_factor)).reshape(-1, wconv_total.shape[1])
    if not steps:
        buf = (buf * jnp.float32(norm_factor)).reshape(-1, wconv_total.shape[1])
    early.extend(item[0] for item in pending)
    if sent_rows < positions:
        late.append(send_rows((lower_all, upper_all), sent_rows, positions))
    received = early + late
    received_ahead = jnp.concatenate([pair[0] for pair in received], axis=0)
    received_behind = jnp.concatenate([pair[1] for pair in received], axis=0)
    total_sum = cotangent.astype(jnp.float32) + jnp.concatenate(mids, axis=0)
    total_sum = total_sum + received_ahead.astype(jnp.float32) + received_behind.astype(jnp.float32)
    grad_input = total_sum.astype(jnp.bfloat16)
    split = wconv_total.shape[0]
    grad_conv = buf[:split]
    grad_out = buf[split:].reshape(wout_total.shape)
    return grad_input, grad_conv, grad_out


def solution(mesh):
    in_specs = (P(("grp", "seq"), None), P(("grp", "seq"), None), P(), P())
    out_specs = (P(("grp", "seq"), None), P("grp", None), P("grp", None))
    return jax.shard_map(body, mesh=mesh, in_specs=in_specs, out_specs=out_specs, check_vma=False)
```

```python
import math

import jax
import jax.numpy as jnp
from jax import lax
from jax.sharding import PartitionSpec as P

TAP_SPACING = 16384
CHUNK_EIGHTHS = (2, 2, 2, 1, 1)
EARLY = 1
RIDER_ROWS = 512
RIDER_SPAN = 2
LATE_PARTS = 1


def from_behind(value, axis, steps):
    count = lax.axis_size(axis)
    pairs = [(source, (source + steps) % count) for source in range(count)]
    return lax.ppermute(value, axis, pairs)


def exchange(value, axis, bit):
    count = lax.axis_size(axis)
    pairs = [(source, source ^ bit) for source in range(count)]
    return lax.ppermute(value, axis, pairs)


def chain_steps(count):
    bits = []
    bit = 1
    while bit < count:
        bits.append(bit)
        bit *= 2
    return [(bit, True) for bit in bits] + [(bit, False) for bit in reversed(bits)]


def chain_step(buf, axis, bit, down):
    idx = lax.axis_index(axis)
    upper = (idx // bit) % 2
    if down:
        half = buf.shape[0] // 2
        mine = lax.dynamic_slice_in_dim(buf, upper * half, half)
        theirs = lax.dynamic_slice_in_dim(buf, (1 - upper) * half, half)
        return mine + exchange(theirs, axis, bit)
    other = exchange(buf, axis, bit)
    lo = jnp.where(upper == 1, other, buf)
    hi = jnp.where(upper == 1, buf, other)
    return jnp.concatenate([lo, hi])


def chunk_layer(left_tap_input, middle, right_tap_input, grad_in, conv_weight, out_weight):
    channels = middle.shape[1]
    w_low = conv_weight[:channels]
    w_mid = conv_weight[channels : 2 * channels]
    w_high = conv_weight[2 * channels :]
    preact = jnp.dot(left_tap_input, w_low, preferred_element_type=jnp.float32)
    preact = preact + jnp.dot(middle, w_mid, preferred_element_type=jnp.float32)
    preact = preact + jnp.dot(right_tap_input, w_high, preferred_element_type=jnp.float32)
    tanh_part = jnp.tanh(preact[:, :channels])
    sigm_part = jax.nn.sigmoid(preact[:, channels:])
    gated_out = (tanh_part * sigm_part).astype(jnp.bfloat16)
    first_dims = (((0,), (0,)), ((), ()))
    last_dims = (((1,), (1,)), ((), ()))
    grad_wout = lax.dot_general(gated_out, grad_in, first_dims, preferred_element_type=jnp.float32)
    grad_gated = lax.dot_general(grad_in, out_weight, last_dims, preferred_element_type=jnp.float32)
    grad_filt = grad_gated * sigm_part * (1.0 - tanh_part * tanh_part)
    grad_gate = grad_gated * tanh_part * sigm_part * (1.0 - sigm_part)
    grad_pre = jnp.concatenate([grad_filt, grad_gate], axis=1).astype(jnp.bfloat16)
    grad_wconv = jnp.concatenate(
        [
            lax.dot_general(left_tap_input, grad_pre, first_dims, preferred_element_type=jnp.float32),
            lax.dot_general(middle, grad_pre, first_dims, preferred_element_type=jnp.float32),
            lax.dot_general(right_tap_input, grad_pre, first_dims, preferred_element_type=jnp.float32),
        ],
        axis=0,
    )
    lower_term = lax.dot_general(grad_pre, w_low, last_dims, preferred_element_type=jnp.float32).astype(jnp.bfloat16)
    term_mid = lax.dot_general(grad_pre, w_mid, last_dims, preferred_element_type=jnp.float32)
    upper_term = lax.dot_general(grad_pre, w_high, last_dims, preferred_element_type=jnp.float32).astype(jnp.bfloat16)
    return grad_wconv, grad_wout, lower_term, term_mid, upper_term


def body(activations, cotangent, conv_weight, out_weight):
    positions, channels = activations.shape
    seq_size = lax.axis_size("seq")
    spacing = TAP_SPACING // positions
    bounds = [0]
    for eighths in CHUNK_EIGHTHS:
        bounds.append(bounds[-1] + positions * eighths // 8)
    chunks = len(CHUNK_EIGHTHS)
    wconv_total = None
    wout_total = None
    lows, mids, highs = [], [], []
    early = []
    for k in range(chunks):
        middle = activations[bounds[k] : bounds[k + 1]]
        grad_in = cotangent[bounds[k] : bounds[k + 1]]
        left_tap_input = from_behind(middle, "seq", spacing)
        right_tap_input = from_behind(middle, "seq", -spacing)
        if k == chunks - 1:
            left_tap_input, right_tap_input, lows_early, highs_early = lax.optimization_barrier(
                (left_tap_input, right_tap_input, lows[:EARLY], highs[:EARLY])
            )
            for low, high in zip(lows_early, highs_early):
                half = low.shape[0] // 2
                for part in (slice(0, half), slice(half, low.shape[0])):
                    early.append((from_behind(low[part], "seq", -spacing), from_behind(high[part], "seq", spacing)))
        if wconv_total is not None:
            left_tap_input, right_tap_input, wconv_total, wout_total = lax.optimization_barrier(
                (left_tap_input, right_tap_input, wconv_total, wout_total)
            )
        grad_wconv, grad_wout, lower_term, term_mid, upper_term = chunk_layer(
            left_tap_input, middle, right_tap_input, grad_in, conv_weight, out_weight
        )
        wconv_total = grad_wconv if wconv_total is None else wconv_total + grad_wconv
        wout_total = grad_wout if wout_total is None else wout_total + grad_wout
        lows.append(lower_term)
        mids.append(term_mid)
        highs.append(upper_term)
    norm_factor = 1.0 / math.sqrt(positions * seq_size)
    buf = jnp.concatenate([wconv_total.reshape(-1), wout_total.reshape(-1)])
    lower_all = jnp.concatenate(lows, axis=0)
    upper_all = jnp.concatenate(highs, axis=0)

    def send_rows(low_high, start, stop):
        return (
            from_behind(low_high[0][start:stop], "seq", -spacing),
            from_behind(low_high[1][start:stop], "seq", spacing),
        )

    steps = chain_steps(seq_size)
    rider_steps = [(4, True), (8, True), (8, False), (4, False)]
    sent_rows = bounds[EARLY]
    pending = []
    late = []
    for number, (bit, down) in enumerate(steps):
        if down and bit == 4:
            buf, early = lax.optimization_barrier((buf, early))
        due = [item for item in pending if item[1] <= number]
        if due:
            buf, landed = lax.optimization_barrier((buf, [item[0] for item in due]))
            early.extend(landed)
            pending = [item for item in pending if item[1] > number]
        if (bit, down) in rider_steps and sent_rows + RIDER_ROWS <= positions:
            buf, pieces = lax.optimization_barrier((buf, (lower_all, upper_all)))
            pending.append((send_rows(pieces, sent_rows, sent_rows + RIDER_ROWS), number + RIDER_SPAN))
            sent_rows += RIDER_ROWS
        if not down and bit == 2 and not late:
            buf, pieces = lax.optimization_barrier((buf, (lower_all, upper_all)))
            for part in range(LATE_PARTS):
                start = sent_rows + part * (positions - sent_rows) // LATE_PARTS
                stop = sent_rows + (part + 1) * (positions - sent_rows) // LATE_PARTS
                late.append(send_rows(pieces, start, stop))
            sent_rows = positions
        if not down and bit == 1 and late:
            buf, late = lax.optimization_barrier((buf, late))
        buf = chain_step(buf, "seq", bit, down)
        if down and number == len(steps) // 2 - 1:
            buf = (buf * jnp.float32(norm_factor)).reshape(-1, wconv_total.shape[1])
    if not steps:
        buf = (buf * jnp.float32(norm_factor)).reshape(-1, wconv_total.shape[1])
    early.extend(item[0] for item in pending)
    if sent_rows < positions:
        late.append(send_rows((lower_all, upper_all), sent_rows, positions))
    received = early + late
    received_ahead = jnp.concatenate([pair[0] for pair in received], axis=0)
    received_behind = jnp.concatenate([pair[1] for pair in received], axis=0)
    total_sum = cotangent.astype(jnp.float32) + jnp.concatenate(mids, axis=0)
    total_sum = total_sum + received_ahead.astype(jnp.float32) + received_behind.astype(jnp.float32)
    grad_input = total_sum.astype(jnp.bfloat16)
    split = wconv_total.shape[0]
    grad_conv = buf[:split]
    grad_out = buf[split:].reshape(wout_total.shape)
    return grad_input, grad_conv, grad_out


def solution(mesh):
    in_specs = (P(("grp", "seq"), None), P(("grp", "seq"), None), P(), P())
    out_specs = (P(("grp", "seq"), None), P("grp", None), P("grp", None))
    return jax.shard_map(body, mesh=mesh, in_specs=in_specs, out_specs=out_specs, check_vma=False)
```

```python
import math

import jax
import jax.numpy as jnp
from jax import lax
from jax.sharding import PartitionSpec as P

TAP_SPACING = 16384
CHUNK_EIGHTHS = (2, 2, 2, 1, 1)
EARLY = 1
RIDER_ROWS = 512
RIDER_SPAN = 2
LATE_PARTS = 4


def from_behind(value, axis, steps):
    count = lax.axis_size(axis)
    pairs = [(source, (source + steps) % count) for source in range(count)]
    return lax.ppermute(value, axis, pairs)


def exchange(value, axis, bit):
    count = lax.axis_size(axis)
    pairs = [(source, source ^ bit) for source in range(count)]
    return lax.ppermute(value, axis, pairs)


def chain_steps(count):
    bits = []
    bit = 1
    while bit < count:
        bits.append(bit)
        bit *= 2
    return [(bit, True) for bit in bits] + [(bit, False) for bit in reversed(bits)]


def chain_step(buf, axis, bit, down):
    idx = lax.axis_index(axis)
    upper = (idx // bit) % 2
    if down:
        half = buf.shape[0] // 2
        mine = lax.dynamic_slice_in_dim(buf, upper * half, half)
        theirs = lax.dynamic_slice_in_dim(buf, (1 - upper) * half, half)
        return mine + exchange(theirs, axis, bit)
    other = exchange(buf, axis, bit)
    lo = jnp.where(upper == 1, other, buf)
    hi = jnp.where(upper == 1, buf, other)
    return jnp.concatenate([lo, hi])


def chunk_layer(left_tap_input, middle, right_tap_input, grad_in, conv_weight, out_weight):
    channels = middle.shape[1]
    w_low = conv_weight[:channels]
    w_mid = conv_weight[channels : 2 * channels]
    w_high = conv_weight[2 * channels :]
    preact = jnp.dot(left_tap_input, w_low, preferred_element_type=jnp.float32)
    preact = preact + jnp.dot(middle, w_mid, preferred_element_type=jnp.float32)
    preact = preact + jnp.dot(right_tap_input, w_high, preferred_element_type=jnp.float32)
    tanh_part = jnp.tanh(preact[:, :channels])
    sigm_part = jax.nn.sigmoid(preact[:, channels:])
    gated_out = (tanh_part * sigm_part).astype(jnp.bfloat16)
    first_dims = (((0,), (0,)), ((), ()))
    last_dims = (((1,), (1,)), ((), ()))
    grad_wout = lax.dot_general(gated_out, grad_in, first_dims, preferred_element_type=jnp.float32)
    grad_gated = lax.dot_general(grad_in, out_weight, last_dims, preferred_element_type=jnp.float32)
    grad_filt = grad_gated * sigm_part * (1.0 - tanh_part * tanh_part)
    grad_gate = grad_gated * tanh_part * sigm_part * (1.0 - sigm_part)
    grad_pre = jnp.concatenate([grad_filt, grad_gate], axis=1).astype(jnp.bfloat16)
    grad_wconv = jnp.concatenate(
        [
            lax.dot_general(left_tap_input, grad_pre, first_dims, preferred_element_type=jnp.float32),
            lax.dot_general(middle, grad_pre, first_dims, preferred_element_type=jnp.float32),
            lax.dot_general(right_tap_input, grad_pre, first_dims, preferred_element_type=jnp.float32),
        ],
        axis=0,
    )
    lower_term = lax.dot_general(grad_pre, w_low, last_dims, preferred_element_type=jnp.float32).astype(jnp.bfloat16)
    term_mid = lax.dot_general(grad_pre, w_mid, last_dims, preferred_element_type=jnp.float32)
    upper_term = lax.dot_general(grad_pre, w_high, last_dims, preferred_element_type=jnp.float32).astype(jnp.bfloat16)
    return grad_wconv, grad_wout, lower_term, term_mid, upper_term


def body(activations, cotangent, conv_weight, out_weight):
    positions, channels = activations.shape
    seq_size = lax.axis_size("seq")
    spacing = TAP_SPACING // positions
    bounds = [0]
    for eighths in CHUNK_EIGHTHS:
        bounds.append(bounds[-1] + positions * eighths // 8)
    chunks = len(CHUNK_EIGHTHS)
    wconv_total = None
    wout_total = None
    lows, mids, highs = [], [], []
    early = []
    for k in range(chunks):
        middle = activations[bounds[k] : bounds[k + 1]]
        grad_in = cotangent[bounds[k] : bounds[k + 1]]
        left_tap_input = from_behind(middle, "seq", spacing)
        right_tap_input = from_behind(middle, "seq", -spacing)
        if k == chunks - 1:
            left_tap_input, right_tap_input, lows_early, highs_early = lax.optimization_barrier(
                (left_tap_input, right_tap_input, lows[:EARLY], highs[:EARLY])
            )
            for low, high in zip(lows_early, highs_early):
                half = low.shape[0] // 2
                for part in (slice(0, half), slice(half, low.shape[0])):
                    early.append((from_behind(low[part], "seq", -spacing), from_behind(high[part], "seq", spacing)))
        if wconv_total is not None:
            left_tap_input, right_tap_input, wconv_total, wout_total = lax.optimization_barrier(
                (left_tap_input, right_tap_input, wconv_total, wout_total)
            )
        grad_wconv, grad_wout, lower_term, term_mid, upper_term = chunk_layer(
            left_tap_input, middle, right_tap_input, grad_in, conv_weight, out_weight
        )
        wconv_total = grad_wconv if wconv_total is None else wconv_total + grad_wconv
        wout_total = grad_wout if wout_total is None else wout_total + grad_wout
        lows.append(lower_term)
        mids.append(term_mid)
        highs.append(upper_term)
    norm_factor = 1.0 / math.sqrt(positions * seq_size)
    buf = jnp.concatenate([wconv_total.reshape(-1), wout_total.reshape(-1)])
    lower_all = jnp.concatenate(lows, axis=0)
    upper_all = jnp.concatenate(highs, axis=0)

    def send_rows(low_high, start, stop):
        return (
            from_behind(low_high[0][start:stop], "seq", -spacing),
            from_behind(low_high[1][start:stop], "seq", spacing),
        )

    steps = chain_steps(seq_size)
    rider_steps = [(4, True), (8, True), (8, False), (4, False)]
    sent_rows = bounds[EARLY]
    pending = []
    late = []
    for number, (bit, down) in enumerate(steps):
        if down and bit == 4:
            buf, early = lax.optimization_barrier((buf, early))
        due = [item for item in pending if item[1] <= number]
        if due:
            buf, landed = lax.optimization_barrier((buf, [item[0] for item in due]))
            early.extend(landed)
            pending = [item for item in pending if item[1] > number]
        if (bit, down) in rider_steps and sent_rows + RIDER_ROWS <= positions:
            buf, pieces = lax.optimization_barrier((buf, (lower_all, upper_all)))
            pending.append((send_rows(pieces, sent_rows, sent_rows + RIDER_ROWS), number + RIDER_SPAN))
            sent_rows += RIDER_ROWS
        if not down and bit == 2 and not late:
            buf, pieces = lax.optimization_barrier((buf, (lower_all, upper_all)))
            for part in range(LATE_PARTS):
                start = sent_rows + part * (positions - sent_rows) // LATE_PARTS
                stop = sent_rows + (part + 1) * (positions - sent_rows) // LATE_PARTS
                late.append(send_rows(pieces, start, stop))
            sent_rows = positions
        if not down and bit == 1 and late:
            buf, late = lax.optimization_barrier((buf, late))
        buf = chain_step(buf, "seq", bit, down)
        if down and number == len(steps) // 2 - 1:
            buf = (buf * jnp.float32(norm_factor)).reshape(-1, wconv_total.shape[1])
    if not steps:
        buf = (buf * jnp.float32(norm_factor)).reshape(-1, wconv_total.shape[1])
    early.extend(item[0] for item in pending)
    if sent_rows < positions:
        late.append(send_rows((lower_all, upper_all), sent_rows, positions))
    received = early + late
    received_ahead = jnp.concatenate([pair[0] for pair in received], axis=0)
    received_behind = jnp.concatenate([pair[1] for pair in received], axis=0)
    total_sum = cotangent.astype(jnp.float32) + jnp.concatenate(mids, axis=0)
    total_sum = total_sum + received_ahead.astype(jnp.float32) + received_behind.astype(jnp.float32)
    grad_input = total_sum.astype(jnp.bfloat16)
    split = wconv_total.shape[0]
    grad_conv = buf[:split]
    grad_out = buf[split:].reshape(wout_total.shape)
    return grad_input, grad_conv, grad_out


def solution(mesh):
    in_specs = (P(("grp", "seq"), None), P(("grp", "seq"), None), P(), P())
    out_specs = (P(("grp", "seq"), None), P("grp", None), P("grp", None))
    return jax.shard_map(body, mesh=mesh, in_specs=in_specs, out_specs=out_specs, check_vma=False)
```

```python
import math

import jax
import jax.numpy as jnp
from jax import lax
from jax.sharding import PartitionSpec as P

TAP_SPACING = 16384
CHUNK_EIGHTHS = (2, 2, 2, 1, 1)
EARLY = 1
RIDER_ROWS = 512
RIDER_SPANS = (1, 2, 2, 2)


def from_behind(value, axis, steps):
    count = lax.axis_size(axis)
    pairs = [(source, (source + steps) % count) for source in range(count)]
    return lax.ppermute(value, axis, pairs)


def exchange(value, axis, bit):
    count = lax.axis_size(axis)
    pairs = [(source, source ^ bit) for source in range(count)]
    return lax.ppermute(value, axis, pairs)


def chain_steps(count):
    bits = []
    bit = 1
    while bit < count:
        bits.append(bit)
        bit *= 2
    return [(bit, True) for bit in bits] + [(bit, False) for bit in reversed(bits)]


def chain_step(buf, axis, bit, down):
    idx = lax.axis_index(axis)
    upper = (idx // bit) % 2
    if down:
        half = buf.shape[0] // 2
        mine = lax.dynamic_slice_in_dim(buf, upper * half, half)
        theirs = lax.dynamic_slice_in_dim(buf, (1 - upper) * half, half)
        return mine + exchange(theirs, axis, bit)
    other = exchange(buf, axis, bit)
    lo = jnp.where(upper == 1, other, buf)
    hi = jnp.where(upper == 1, buf, other)
    return jnp.concatenate([lo, hi])


def chunk_layer(left_tap_input, middle, right_tap_input, grad_in, conv_weight, out_weight):
    channels = middle.shape[1]
    w_low = conv_weight[:channels]
    w_mid = conv_weight[channels : 2 * channels]
    w_high = conv_weight[2 * channels :]
    preact = jnp.dot(left_tap_input, w_low, preferred_element_type=jnp.float32)
    preact = preact + jnp.dot(middle, w_mid, preferred_element_type=jnp.float32)
    preact = preact + jnp.dot(right_tap_input, w_high, preferred_element_type=jnp.float32)
    tanh_part = jnp.tanh(preact[:, :channels])
    sigm_part = jax.nn.sigmoid(preact[:, channels:])
    gated_out = (tanh_part * sigm_part).astype(jnp.bfloat16)
    first_dims = (((0,), (0,)), ((), ()))
    last_dims = (((1,), (1,)), ((), ()))
    grad_wout = lax.dot_general(gated_out, grad_in, first_dims, preferred_element_type=jnp.float32)
    grad_gated = lax.dot_general(grad_in, out_weight, last_dims, preferred_element_type=jnp.float32)
    grad_filt = grad_gated * sigm_part * (1.0 - tanh_part * tanh_part)
    grad_gate = grad_gated * tanh_part * sigm_part * (1.0 - sigm_part)
    grad_pre = jnp.concatenate([grad_filt, grad_gate], axis=1).astype(jnp.bfloat16)
    grad_wconv = jnp.concatenate(
        [
            lax.dot_general(left_tap_input, grad_pre, first_dims, preferred_element_type=jnp.float32),
            lax.dot_general(middle, grad_pre, first_dims, preferred_element_type=jnp.float32),
            lax.dot_general(right_tap_input, grad_pre, first_dims, preferred_element_type=jnp.float32),
        ],
        axis=0,
    )
    lower_term = lax.dot_general(grad_pre, w_low, last_dims, preferred_element_type=jnp.float32).astype(jnp.bfloat16)
    term_mid = lax.dot_general(grad_pre, w_mid, last_dims, preferred_element_type=jnp.float32)
    upper_term = lax.dot_general(grad_pre, w_high, last_dims, preferred_element_type=jnp.float32).astype(jnp.bfloat16)
    return grad_wconv, grad_wout, lower_term, term_mid, upper_term


def body(activations, cotangent, conv_weight, out_weight):
    positions, channels = activations.shape
    seq_size = lax.axis_size("seq")
    spacing = TAP_SPACING // positions
    bounds = [0]
    for eighths in CHUNK_EIGHTHS:
        bounds.append(bounds[-1] + positions * eighths // 8)
    chunks = len(CHUNK_EIGHTHS)
    wconv_total = None
    wout_total = None
    lows, mids, highs = [], [], []
    early = []
    for k in range(chunks):
        middle = activations[bounds[k] : bounds[k + 1]]
        grad_in = cotangent[bounds[k] : bounds[k + 1]]
        left_tap_input = from_behind(middle, "seq", spacing)
        right_tap_input = from_behind(middle, "seq", -spacing)
        if k == chunks - 1:
            left_tap_input, right_tap_input, lows_early, highs_early = lax.optimization_barrier(
                (left_tap_input, right_tap_input, lows[:EARLY], highs[:EARLY])
            )
            for low, high in zip(lows_early, highs_early):
                half = low.shape[0] // 2
                for part in (slice(0, half), slice(half, low.shape[0])):
                    early.append((from_behind(low[part], "seq", -spacing), from_behind(high[part], "seq", spacing)))
        if wconv_total is not None:
            left_tap_input, right_tap_input, wconv_total, wout_total = lax.optimization_barrier(
                (left_tap_input, right_tap_input, wconv_total, wout_total)
            )
        grad_wconv, grad_wout, lower_term, term_mid, upper_term = chunk_layer(
            left_tap_input, middle, right_tap_input, grad_in, conv_weight, out_weight
        )
        wconv_total = grad_wconv if wconv_total is None else wconv_total + grad_wconv
        wout_total = grad_wout if wout_total is None else wout_total + grad_wout
        lows.append(lower_term)
        mids.append(term_mid)
        highs.append(upper_term)
    norm_factor = 1.0 / math.sqrt(positions * seq_size)
    buf = jnp.concatenate([wconv_total.reshape(-1), wout_total.reshape(-1)])
    lower_all = jnp.concatenate(lows, axis=0)
    upper_all = jnp.concatenate(highs, axis=0)

    def send_rows(low_high, start, stop):
        return (
            from_behind(low_high[0][start:stop], "seq", -spacing),
            from_behind(low_high[1][start:stop], "seq", spacing),
        )

    steps = chain_steps(seq_size)
    rider_steps = [(4, True), (8, True), (8, False), (4, False)]
    sent_rows = bounds[EARLY]
    pending = []
    late = []
    riders_sent = 0
    for number, (bit, down) in enumerate(steps):
        if down and bit == 4:
            buf, early = lax.optimization_barrier((buf, early))
        due = [item for item in pending if item[1] <= number]
        if due:
            buf, landed = lax.optimization_barrier((buf, [item[0] for item in due]))
            early.extend(landed)
            pending = [item for item in pending if item[1] > number]
        if (bit, down) in rider_steps and sent_rows + RIDER_ROWS <= positions:
            buf, pieces = lax.optimization_barrier((buf, (lower_all, upper_all)))
            span = RIDER_SPANS[min(riders_sent, len(RIDER_SPANS) - 1)]
            riders_sent += 1
            pending.append((send_rows(pieces, sent_rows, sent_rows + RIDER_ROWS), number + span))
            sent_rows += RIDER_ROWS
        if not down and bit == 2 and not late:
            buf, pieces = lax.optimization_barrier((buf, (lower_all, upper_all)))
            middle_row = sent_rows + (positions - sent_rows) // 2
            late.append(send_rows(pieces, sent_rows, middle_row))
            late.append(send_rows(pieces, middle_row, positions))
            sent_rows = positions
        if not down and bit == 1 and late:
            buf, late = lax.optimization_barrier((buf, late))
        buf = chain_step(buf, "seq", bit, down)
        if down and number == len(steps) // 2 - 1:
            buf = (buf * jnp.float32(norm_factor)).reshape(-1, wconv_total.shape[1])
    if not steps:
        buf = (buf * jnp.float32(norm_factor)).reshape(-1, wconv_total.shape[1])
    early.extend(item[0] for item in pending)
    if sent_rows < positions:
        late.append(send_rows((lower_all, upper_all), sent_rows, positions))
    received = early + late
    received_ahead = jnp.concatenate([pair[0] for pair in received], axis=0)
    received_behind = jnp.concatenate([pair[1] for pair in received], axis=0)
    total_sum = cotangent.astype(jnp.float32) + jnp.concatenate(mids, axis=0)
    total_sum = total_sum + received_ahead.astype(jnp.float32) + received_behind.astype(jnp.float32)
    grad_input = total_sum.astype(jnp.bfloat16)
    split = wconv_total.shape[0]
    grad_conv = buf[:split]
    grad_out = buf[split:].reshape(wout_total.shape)
    return grad_input, grad_conv, grad_out


def solution(mesh):
    in_specs = (P(("grp", "seq"), None), P(("grp", "seq"), None), P(), P())
    out_specs = (P(("grp", "seq"), None), P("grp", None), P("grp", None))
    return jax.shard_map(body, mesh=mesh, in_specs=in_specs, out_specs=out_specs, check_vma=False)
```

```python
import math

import jax
import jax.numpy as jnp
from jax import lax
from jax.sharding import PartitionSpec as P

TAP_SPACING = 16384
CHUNK_EIGHTHS = (2, 2, 2, 1, 1)
EARLY = 1
RIDER_ROWS = 512
RIDER_SPAN = 2


def from_behind(value, axis, steps):
    count = lax.axis_size(axis)
    pairs = [(source, (source + steps) % count) for source in range(count)]
    return lax.ppermute(value, axis, pairs)


def exchange(value, axis, bit):
    count = lax.axis_size(axis)
    pairs = [(source, source ^ bit) for source in range(count)]
    return lax.ppermute(value, axis, pairs)


def chain_steps(count):
    bits = []
    bit = 1
    while bit < count:
        bits.append(bit)
        bit *= 2
    return [(bit, True) for bit in bits] + [(bit, False) for bit in reversed(bits)]


def chain_step(buf, axis, bit, down):
    idx = lax.axis_index(axis)
    upper = (idx // bit) % 2
    if down:
        half = buf.shape[0] // 2
        mine = lax.dynamic_slice_in_dim(buf, upper * half, half)
        theirs = lax.dynamic_slice_in_dim(buf, (1 - upper) * half, half)
        return mine + exchange(theirs, axis, bit)
    other = exchange(buf, axis, bit)
    lo = jnp.where(upper == 1, other, buf)
    hi = jnp.where(upper == 1, buf, other)
    return jnp.concatenate([lo, hi])


def chunk_layer(left_tap_input, middle, right_tap_input, grad_in, conv_weight, out_weight):
    channels = middle.shape[1]
    w_low = conv_weight[:channels]
    w_mid = conv_weight[channels : 2 * channels]
    w_high = conv_weight[2 * channels :]
    preact = jnp.dot(left_tap_input, w_low, preferred_element_type=jnp.float32)
    preact = preact + jnp.dot(middle, w_mid, preferred_element_type=jnp.float32)
    preact = preact + jnp.dot(right_tap_input, w_high, preferred_element_type=jnp.float32)
    tanh_part = jnp.tanh(preact[:, :channels])
    sigm_part = jax.nn.sigmoid(preact[:, channels:])
    gated_out = (tanh_part * sigm_part).astype(jnp.bfloat16)
    first_dims = (((0,), (0,)), ((), ()))
    last_dims = (((1,), (1,)), ((), ()))
    grad_wout = lax.dot_general(gated_out, grad_in, first_dims, preferred_element_type=jnp.float32)
    grad_gated = lax.dot_general(grad_in, out_weight, last_dims, preferred_element_type=jnp.float32)
    grad_filt = grad_gated * sigm_part * (1.0 - tanh_part * tanh_part)
    grad_gate = grad_gated * tanh_part * sigm_part * (1.0 - sigm_part)
    grad_pre = jnp.concatenate([grad_filt, grad_gate], axis=1).astype(jnp.bfloat16)
    grad_wconv = jnp.concatenate(
        [
            lax.dot_general(left_tap_input, grad_pre, first_dims, preferred_element_type=jnp.float32),
            lax.dot_general(middle, grad_pre, first_dims, preferred_element_type=jnp.float32),
            lax.dot_general(right_tap_input, grad_pre, first_dims, preferred_element_type=jnp.float32),
        ],
        axis=0,
    )
    lower_term = lax.dot_general(grad_pre, w_low, last_dims, preferred_element_type=jnp.float32).astype(jnp.bfloat16)
    term_mid = lax.dot_general(grad_pre, w_mid, last_dims, preferred_element_type=jnp.float32)
    upper_term = lax.dot_general(grad_pre, w_high, last_dims, preferred_element_type=jnp.float32).astype(jnp.bfloat16)
    return grad_wconv, grad_wout, lower_term, term_mid, upper_term


def body(activations, cotangent, conv_weight, out_weight):
    positions, channels = activations.shape
    seq_size = lax.axis_size("seq")
    spacing = TAP_SPACING // positions
    bounds = [0]
    for eighths in CHUNK_EIGHTHS:
        bounds.append(bounds[-1] + positions * eighths // 8)
    chunks = len(CHUNK_EIGHTHS)
    wconv_total = None
    wout_total = None
    lows, mids, highs = [], [], []
    early = []
    for k in range(chunks):
        middle = activations[bounds[k] : bounds[k + 1]]
        grad_in = cotangent[bounds[k] : bounds[k + 1]]
        left_tap_input = from_behind(middle, "seq", spacing)
        right_tap_input = from_behind(middle, "seq", -spacing)
        if k == chunks - 1:
            left_tap_input, right_tap_input, lows_early, highs_early = lax.optimization_barrier(
                (left_tap_input, right_tap_input, lows[:EARLY], highs[:EARLY])
            )
            for low, high in zip(lows_early, highs_early):
                half = low.shape[0] // 2
                for part in (slice(0, half), slice(half, low.shape[0])):
                    early.append((from_behind(low[part], "seq", -spacing), from_behind(high[part], "seq", spacing)))
        if wconv_total is not None:
            left_tap_input, right_tap_input, wconv_total, wout_total = lax.optimization_barrier(
                (left_tap_input, right_tap_input, wconv_total, wout_total)
            )
        grad_wconv, grad_wout, lower_term, term_mid, upper_term = chunk_layer(
            left_tap_input, middle, right_tap_input, grad_in, conv_weight, out_weight
        )
        wconv_total = grad_wconv if wconv_total is None else wconv_total + grad_wconv
        wout_total = grad_wout if wout_total is None else wout_total + grad_wout
        lows.append(lower_term)
        mids.append(term_mid)
        highs.append(upper_term)
    norm_factor = 1.0 / math.sqrt(positions * seq_size)
    buf = jnp.concatenate([wconv_total.reshape(-1), wout_total.reshape(-1)])
    lower_all = jnp.concatenate(lows, axis=0)
    upper_all = jnp.concatenate(highs, axis=0)

    def send_rows(low_high, start, stop):
        return (
            from_behind(low_high[0][start:stop], "seq", -spacing),
            from_behind(low_high[1][start:stop], "seq", spacing),
        )

    steps = chain_steps(seq_size)
    rider_steps = [(4, True), (8, True), (8, False), (4, False)]
    sent_rows = bounds[EARLY]
    pending = []
    late = []
    finished = None
    head_rows = 0
    head_count = 0
    for number, (bit, down) in enumerate(steps):
        if down and bit == 4:
            buf, early = lax.optimization_barrier((buf, early))
        due = [item for item in pending if item[1] <= number]
        if due:
            buf, landed = lax.optimization_barrier((buf, [item[0] for item in due]))
            early.extend(landed)
            pending = [item for item in pending if item[1] > number]
        if (bit, down) in rider_steps and sent_rows + RIDER_ROWS <= positions:
            buf, pieces = lax.optimization_barrier((buf, (lower_all, upper_all)))
            pending.append((send_rows(pieces, sent_rows, sent_rows + RIDER_ROWS), number + RIDER_SPAN))
            sent_rows += RIDER_ROWS
        if not down and bit == 2 and not late:
            landed = jnp.concatenate([pair[0] for pair in early], axis=0).astype(jnp.float32)
            landed = landed + jnp.concatenate([pair[1] for pair in early], axis=0).astype(jnp.float32)
            head_rows = landed.shape[0]
            head_count = len(early)
            landed = jnp.pad(landed, ((0, positions - head_rows), (0, 0)))
            finished = (cotangent.astype(jnp.float32) + jnp.concatenate(mids, axis=0) + landed).astype(jnp.bfloat16)
            buf, finished = lax.optimization_barrier((buf, finished))
            buf, pieces = lax.optimization_barrier((buf, (lower_all, upper_all)))
            middle_row = sent_rows + (positions - sent_rows) // 2
            late.append(send_rows(pieces, sent_rows, middle_row))
            late.append(send_rows(pieces, middle_row, positions))
            sent_rows = positions
        if not down and bit == 1 and late:
            buf, late = lax.optimization_barrier((buf, late))
        buf = chain_step(buf, "seq", bit, down)
        if down and number == len(steps) // 2 - 1:
            buf = (buf * jnp.float32(norm_factor)).reshape(-1, wconv_total.shape[1])
    if not steps:
        buf = (buf * jnp.float32(norm_factor)).reshape(-1, wconv_total.shape[1])
    early.extend(item[0] for item in pending)
    if sent_rows < positions:
        late.append(send_rows((lower_all, upper_all), sent_rows, positions))
    mids_all = jnp.concatenate(mids, axis=0)
    if finished is not None:
        tail = early[head_count:] + late
        ahead = jnp.concatenate([pair[0] for pair in tail], axis=0)
        behind = jnp.concatenate([pair[1] for pair in tail], axis=0)
        late_sum = cotangent[head_rows:].astype(jnp.float32) + mids_all[head_rows:]
        late_sum = late_sum + ahead.astype(jnp.float32) + behind.astype(jnp.float32)
        grad_input = lax.dynamic_update_slice(finished, late_sum.astype(jnp.bfloat16), (head_rows, 0))
    else:
        received = early + late
        received_ahead = jnp.concatenate([pair[0] for pair in received], axis=0)
        received_behind = jnp.concatenate([pair[1] for pair in received], axis=0)
        total_sum = cotangent.astype(jnp.float32) + mids_all
        total_sum = total_sum + received_ahead.astype(jnp.float32) + received_behind.astype(jnp.float32)
        grad_input = total_sum.astype(jnp.bfloat16)
    split = wconv_total.shape[0]
    grad_conv = buf[:split]
    grad_out = buf[split:].reshape(wout_total.shape)
    return grad_input, grad_conv, grad_out


def solution(mesh):
    in_specs = (P(("grp", "seq"), None), P(("grp", "seq"), None), P(), P())
    out_specs = (P(("grp", "seq"), None), P("grp", None), P("grp", None))
    return jax.shard_map(body, mesh=mesh, in_specs=in_specs, out_specs=out_specs, check_vma=False)
```

```python
import math

import jax
import jax.numpy as jnp
from jax import lax
from jax.sharding import PartitionSpec as P

TAP_SPACING = 16384
CHUNK_EIGHTHS = (2, 2, 2, 1, 1)
EARLY = 1
RIDER_ROWS = 512
RIDER_SPAN = 2


def from_behind(value, axis, steps):
    count = lax.axis_size(axis)
    pairs = [(source, (source + steps) % count) for source in range(count)]
    return lax.ppermute(value, axis, pairs)


def exchange(value, axis, bit):
    count = lax.axis_size(axis)
    pairs = [(source, source ^ bit) for source in range(count)]
    return lax.ppermute(value, axis, pairs)


def chain_steps(count):
    bits = []
    bit = 1
    while bit < count:
        bits.append(bit)
        bit *= 2
    return [(bit, True) for bit in bits] + [(bit, False) for bit in reversed(bits)]


def chain_step(buf, axis, bit, down):
    idx = lax.axis_index(axis)
    upper = (idx // bit) % 2
    if down:
        half = buf.shape[0] // 2
        mine = lax.dynamic_slice_in_dim(buf, upper * half, half)
        theirs = lax.dynamic_slice_in_dim(buf, (1 - upper) * half, half)
        return mine + exchange(theirs, axis, bit)
    other = exchange(buf, axis, bit)
    lo = jnp.where(upper == 1, other, buf)
    hi = jnp.where(upper == 1, buf, other)
    return jnp.concatenate([lo, hi])


def chunk_layer(left_tap_input, middle, right_tap_input, grad_in, conv_weight, out_weight):
    channels = middle.shape[1]
    w_low = conv_weight[:channels]
    w_mid = conv_weight[channels : 2 * channels]
    w_high = conv_weight[2 * channels :]
    preact = jnp.dot(left_tap_input, w_low, preferred_element_type=jnp.float32)
    preact = preact + jnp.dot(middle, w_mid, preferred_element_type=jnp.float32)
    preact = preact + jnp.dot(right_tap_input, w_high, preferred_element_type=jnp.float32)
    tanh_part = jnp.tanh(preact[:, :channels])
    sigm_part = jax.nn.sigmoid(preact[:, channels:])
    gated_out = (tanh_part * sigm_part).astype(jnp.bfloat16)
    first_dims = (((0,), (0,)), ((), ()))
    last_dims = (((1,), (1,)), ((), ()))
    grad_wout = lax.dot_general(gated_out, grad_in, first_dims, preferred_element_type=jnp.float32)
    grad_gated = lax.dot_general(grad_in, out_weight, last_dims, preferred_element_type=jnp.float32)
    grad_filt = grad_gated * sigm_part * (1.0 - tanh_part * tanh_part)
    grad_gate = grad_gated * tanh_part * sigm_part * (1.0 - sigm_part)
    grad_pre = jnp.concatenate([grad_filt, grad_gate], axis=1).astype(jnp.bfloat16)
    grad_wconv = jnp.concatenate(
        [
            lax.dot_general(left_tap_input, grad_pre, first_dims, preferred_element_type=jnp.float32),
            lax.dot_general(middle, grad_pre, first_dims, preferred_element_type=jnp.float32),
            lax.dot_general(right_tap_input, grad_pre, first_dims, preferred_element_type=jnp.float32),
        ],
        axis=0,
    )
    lower_term = lax.dot_general(grad_pre, w_low, last_dims, preferred_element_type=jnp.float32).astype(jnp.bfloat16)
    term_mid = lax.dot_general(grad_pre, w_mid, last_dims, preferred_element_type=jnp.float32)
    upper_term = lax.dot_general(grad_pre, w_high, last_dims, preferred_element_type=jnp.float32).astype(jnp.bfloat16)
    return grad_wconv, grad_wout, lower_term, term_mid, upper_term


def body(activations, cotangent, conv_weight, out_weight):
    positions, channels = activations.shape
    seq_size = lax.axis_size("seq")
    spacing = TAP_SPACING // positions
    bounds = [0]
    for eighths in CHUNK_EIGHTHS:
        bounds.append(bounds[-1] + positions * eighths // 8)
    chunks = len(CHUNK_EIGHTHS)
    wconv_total = None
    wout_total = None
    lows, mids, highs = [], [], []
    early = []
    for k in range(chunks):
        middle = activations[bounds[k] : bounds[k + 1]]
        grad_in = cotangent[bounds[k] : bounds[k + 1]]
        left_tap_input = from_behind(middle, "seq", spacing)
        right_tap_input = from_behind(middle, "seq", -spacing)
        if k == chunks - 1:
            left_tap_input, right_tap_input, lows_early, highs_early = lax.optimization_barrier(
                (left_tap_input, right_tap_input, lows[:EARLY], highs[:EARLY])
            )
            for low, high in zip(lows_early, highs_early):
                early.append((from_behind(low, "seq", -spacing), from_behind(high, "seq", spacing)))
        if wconv_total is not None:
            left_tap_input, right_tap_input, wconv_total, wout_total = lax.optimization_barrier(
                (left_tap_input, right_tap_input, wconv_total, wout_total)
            )
        grad_wconv, grad_wout, lower_term, term_mid, upper_term = chunk_layer(
            left_tap_input, middle, right_tap_input, grad_in, conv_weight, out_weight
        )
        wconv_total = grad_wconv if wconv_total is None else wconv_total + grad_wconv
        wout_total = grad_wout if wout_total is None else wout_total + grad_wout
        lows.append(lower_term)
        mids.append(term_mid)
        highs.append(upper_term)
    norm_factor = 1.0 / math.sqrt(positions * seq_size)
    buf = jnp.concatenate([wconv_total.reshape(-1), wout_total.reshape(-1)])
    lower_all = jnp.concatenate(lows, axis=0)
    upper_all = jnp.concatenate(highs, axis=0)

    def send_rows(low_high, start, stop):
        return (
            from_behind(low_high[0][start:stop], "seq", -spacing),
            from_behind(low_high[1][start:stop], "seq", spacing),
        )

    steps = chain_steps(seq_size)
    rider_steps = [(4, True), (8, True), (8, False), (4, False)]
    sent_rows = bounds[EARLY]
    pending = []
    late = []
    for number, (bit, down) in enumerate(steps):
        if down and bit == 4:
            buf, early = lax.optimization_barrier((buf, early))
        due = [item for item in pending if item[1] <= number]
        if due:
            buf, landed = lax.optimization_barrier((buf, [item[0] for item in due]))
            early.extend(landed)
            pending = [item for item in pending if item[1] > number]
        if (bit, down) in rider_steps and sent_rows + RIDER_ROWS <= positions:
            buf, pieces = lax.optimization_barrier((buf, (lower_all, upper_all)))
            pending.append((send_rows(pieces, sent_rows, sent_rows + RIDER_ROWS), number + RIDER_SPAN))
            sent_rows += RIDER_ROWS
        if not down and bit == 2 and not late:
            buf, pieces = lax.optimization_barrier((buf, (lower_all, upper_all)))
            middle_row = sent_rows + (positions - sent_rows) // 2
            late.append(send_rows(pieces, sent_rows, middle_row))
            late.append(send_rows(pieces, middle_row, positions))
            sent_rows = positions
        if not down and bit == 1 and late:
            buf, late = lax.optimization_barrier((buf, late))
        buf = chain_step(buf, "seq", bit, down)
        if down and number == len(steps) // 2 - 1:
            buf = (buf * jnp.float32(norm_factor)).reshape(-1, wconv_total.shape[1])
    if not steps:
        buf = (buf * jnp.float32(norm_factor)).reshape(-1, wconv_total.shape[1])
    early.extend(item[0] for item in pending)
    if sent_rows < positions:
        late.append(send_rows((lower_all, upper_all), sent_rows, positions))
    received = early + late
    received_ahead = jnp.concatenate([pair[0] for pair in received], axis=0)
    received_behind = jnp.concatenate([pair[1] for pair in received], axis=0)
    total_sum = cotangent.astype(jnp.float32) + jnp.concatenate(mids, axis=0)
    total_sum = total_sum + received_ahead.astype(jnp.float32) + received_behind.astype(jnp.float32)
    grad_input = total_sum.astype(jnp.bfloat16)
    split = wconv_total.shape[0]
    grad_conv = buf[:split]
    grad_out = buf[split:].reshape(wout_total.shape)
    return grad_input, grad_conv, grad_out


def solution(mesh):
    in_specs = (P(("grp", "seq"), None), P(("grp", "seq"), None), P(), P())
    out_specs = (P(("grp", "seq"), None), P("grp", None), P("grp", None))
    return jax.shard_map(body, mesh=mesh, in_specs=in_specs, out_specs=out_specs, check_vma=False)
```

```python
import math

import jax
import jax.numpy as jnp
from jax import lax
from jax.sharding import PartitionSpec as P

TAP_SPACING = 16384
CHUNK_EIGHTHS = (2, 2, 2, 1, 1)
EARLY = 1
RIDER_ROWS = 512
RIDER_SPAN = 2


def from_behind(value, axis, steps):
    count = lax.axis_size(axis)
    pairs = [(source, (source + steps) % count) for source in range(count)]
    return lax.ppermute(value, axis, pairs)


def exchange(value, axis, bit):
    count = lax.axis_size(axis)
    pairs = [(source, source ^ bit) for source in range(count)]
    return lax.ppermute(value, axis, pairs)


def chain_steps(count):
    bits = []
    bit = 1
    while bit < count:
        bits.append(bit)
        bit *= 2
    return [(bit, True) for bit in bits] + [(bit, False) for bit in reversed(bits)]


def chain_step(buf, axis, bit, down):
    idx = lax.axis_index(axis)
    upper = (idx // bit) % 2
    if down:
        half = buf.shape[0] // 2
        mine = lax.dynamic_slice_in_dim(buf, upper * half, half)
        theirs = lax.dynamic_slice_in_dim(buf, (1 - upper) * half, half)
        return mine + exchange(theirs, axis, bit)
    other = exchange(buf, axis, bit)
    lo = jnp.where(upper == 1, other, buf)
    hi = jnp.where(upper == 1, buf, other)
    return jnp.concatenate([lo, hi])


def chunk_layer(left_tap_input, middle, right_tap_input, grad_in, conv_weight, out_weight):
    channels = middle.shape[1]
    w_low = conv_weight[:channels]
    w_mid = conv_weight[channels : 2 * channels]
    w_high = conv_weight[2 * channels :]
    preact = jnp.dot(left_tap_input, w_low, preferred_element_type=jnp.float32)
    preact = preact + jnp.dot(middle, w_mid, preferred_element_type=jnp.float32)
    preact = preact + jnp.dot(right_tap_input, w_high, preferred_element_type=jnp.float32)
    tanh_part = jnp.tanh(preact[:, :channels])
    sigm_part = jax.nn.sigmoid(preact[:, channels:])
    gated_out = (tanh_part * sigm_part).astype(jnp.bfloat16)
    first_dims = (((0,), (0,)), ((), ()))
    last_dims = (((1,), (1,)), ((), ()))
    grad_wout = lax.dot_general(gated_out, grad_in, first_dims, preferred_element_type=jnp.float32)
    grad_gated = lax.dot_general(grad_in, out_weight, last_dims, preferred_element_type=jnp.float32)
    grad_filt = grad_gated * sigm_part * (1.0 - tanh_part * tanh_part)
    grad_gate = grad_gated * tanh_part * sigm_part * (1.0 - sigm_part)
    grad_pre = jnp.concatenate([grad_filt, grad_gate], axis=1).astype(jnp.bfloat16)
    grad_wconv = jnp.concatenate(
        [
            lax.dot_general(left_tap_input, grad_pre, first_dims, preferred_element_type=jnp.float32),
            lax.dot_general(middle, grad_pre, first_dims, preferred_element_type=jnp.float32),
            lax.dot_general(right_tap_input, grad_pre, first_dims, preferred_element_type=jnp.float32),
        ],
        axis=0,
    )
    lower_term = lax.dot_general(grad_pre, w_low, last_dims, preferred_element_type=jnp.float32).astype(jnp.bfloat16)
    term_mid = lax.dot_general(grad_pre, w_mid, last_dims, preferred_element_type=jnp.float32)
    upper_term = lax.dot_general(grad_pre, w_high, last_dims, preferred_element_type=jnp.float32).astype(jnp.bfloat16)
    return grad_wconv, grad_wout, lower_term, term_mid, upper_term


def body(activations, cotangent, conv_weight, out_weight):
    positions, channels = activations.shape
    seq_size = lax.axis_size("seq")
    spacing = TAP_SPACING // positions
    bounds = [0]
    for eighths in CHUNK_EIGHTHS:
        bounds.append(bounds[-1] + positions * eighths // 8)
    chunks = len(CHUNK_EIGHTHS)
    wconv_total = None
    wout_total = None
    lows, mids, highs = [], [], []
    early = []
    for k in range(chunks):
        middle = activations[bounds[k] : bounds[k + 1]]
        grad_in = cotangent[bounds[k] : bounds[k + 1]]
        left_tap_input = from_behind(middle, "seq", spacing)
        right_tap_input = from_behind(middle, "seq", -spacing)
        if k == chunks - 1:
            left_tap_input, right_tap_input, lows_early, highs_early = lax.optimization_barrier(
                (left_tap_input, right_tap_input, lows[:EARLY], highs[:EARLY])
            )
            for low, high in zip(lows_early, highs_early):
                early.append((from_behind(low, "seq", -spacing), from_behind(high, "seq", spacing)))
        if wconv_total is not None:
            left_tap_input, right_tap_input, wconv_total, wout_total = lax.optimization_barrier(
                (left_tap_input, right_tap_input, wconv_total, wout_total)
            )
        grad_wconv, grad_wout, lower_term, term_mid, upper_term = chunk_layer(
            left_tap_input, middle, right_tap_input, grad_in, conv_weight, out_weight
        )
        wconv_total = grad_wconv if wconv_total is None else wconv_total + grad_wconv
        wout_total = grad_wout if wout_total is None else wout_total + grad_wout
        lows.append(lower_term)
        mids.append(term_mid)
        highs.append(upper_term)
    norm_factor = 1.0 / math.sqrt(positions * seq_size)
    buf = jnp.concatenate([wconv_total.reshape(-1), wout_total.reshape(-1)])
    lower_all = jnp.concatenate(lows, axis=0)
    upper_all = jnp.concatenate(highs, axis=0)

    def send_rows(low_high, start, stop):
        return (
            from_behind(low_high[0][start:stop], "seq", -spacing),
            from_behind(low_high[1][start:stop], "seq", spacing),
        )

    steps = chain_steps(seq_size)
    rider_steps = [(4, True), (8, True), (8, False), (4, False)]
    sent_rows = bounds[EARLY]
    pending = []
    late = []
    for number, (bit, down) in enumerate(steps):
        if down and bit == 4:
            buf, early = lax.optimization_barrier((buf, early))
        due = [item for item in pending if item[1] <= number]
        if due:
            buf, landed = lax.optimization_barrier((buf, [item[0] for item in due]))
            early.extend(landed)
            pending = [item for item in pending if item[1] > number]
        if (bit, down) in rider_steps and sent_rows + RIDER_ROWS <= positions:
            buf, pieces = lax.optimization_barrier((buf, (lower_all, upper_all)))
            span = RIDER_SPAN if sent_rows + 2 * RIDER_ROWS <= positions and (bit, down) != rider_steps[-1] else 1
            pending.append((send_rows(pieces, sent_rows, sent_rows + RIDER_ROWS), number + span))
            sent_rows += RIDER_ROWS
        if not down and bit == 2 and not late:
            buf, pieces = lax.optimization_barrier((buf, (lower_all, upper_all)))
            middle_row = sent_rows + (positions - sent_rows) // 2
            late.append(send_rows(pieces, sent_rows, middle_row))
            late.append(send_rows(pieces, middle_row, positions))
            sent_rows = positions
        if not down and bit == 1 and late:
            buf, late = lax.optimization_barrier((buf, late))
        buf = chain_step(buf, "seq", bit, down)
        if down and number == len(steps) // 2 - 1:
            buf = (buf * jnp.float32(norm_factor)).reshape(-1, wconv_total.shape[1])
    if not steps:
        buf = (buf * jnp.float32(norm_factor)).reshape(-1, wconv_total.shape[1])
    early.extend(item[0] for item in pending)
    if sent_rows < positions:
        late.append(send_rows((lower_all, upper_all), sent_rows, positions))
    received = early + late
    received_ahead = jnp.concatenate([pair[0] for pair in received], axis=0)
    received_behind = jnp.concatenate([pair[1] for pair in received], axis=0)
    total_sum = cotangent.astype(jnp.float32) + jnp.concatenate(mids, axis=0)
    total_sum = total_sum + received_ahead.astype(jnp.float32) + received_behind.astype(jnp.float32)
    grad_input = total_sum.astype(jnp.bfloat16)
    split = wconv_total.shape[0]
    grad_conv = buf[:split]
    grad_out = buf[split:].reshape(wout_total.shape)
    return grad_input, grad_conv, grad_out


def solution(mesh):
    in_specs = (P(("grp", "seq"), None), P(("grp", "seq"), None), P(), P())
    out_specs = (P(("grp", "seq"), None), P("grp", None), P("grp", None))
    return jax.shard_map(body, mesh=mesh, in_specs=in_specs, out_specs=out_specs, check_vma=False)
```
